256 devices in a mesh: ctx: 64 (over z, x, core), head: 4 (over y).
Axes of the slice: x: 4, y: 4, z: 8, core: 2. Of those that a mesh axis runs over, the one named last changes fastest.
Arguments:
- queries: bfloat16 [8192, 32, 128], P('ctx', 'head'), may hold values from -14 to 14
- keys: bfloat16 [8192, 32, 128], P('ctx', 'head'), may hold values from -14 to 14
- values: bfloat16 [8192, 32, 128], P('ctx', 'head'), may hold values from -6 to 6
- gain: float32 [32, 128], P('head'), may hold values from 0.1 to 1.9
- doc_lengths: int32 [64], replicated, may hold values from 1 to 2048, 8192 in all
- cotangent: bfloat16 [8192, 32, 128], P('ctx', 'head'), may hold values from -6 to 6
Outputs:
- mixed: bfloat16 [8192, 32, 128], P('ctx', 'head')
- query_grad: bfloat16 [8192, 32, 128], P('ctx', 'head')
- key_grad: bfloat16 [8192, 32, 128], P('ctx', 'head')
- value_grad: bfloat16 [8192, 32, 128], P('ctx', 'head')
The draws below stay inside these ranges and needn't reach their ends.
All inputs are finite; a program needn't handle non-finite values.
Results may differ from the reference program's by a relative error of at most 0.0054.
Values may be sent and summed in bfloat16 or wider, within the bound.
No kernel may reach another device: no remote copies, remote signals or barrier semaphores. Data moves between devices by JAX's collectives and lax.ppermute only.
A program may use at most 128 MiB of HBM per device.

```python
import math
import jax
import jax.numpy as jnp
import numpy as np
from jax import lax

HEADS = 32
DH = 128
TOK_DEV = 128
SPAN = 2
SEQ = 8192
MAXDOC = 2048
NDOCS = 64


def draw_pair(key):
    shape = (SEQ, HEADS, DH)
    first, second = jax.random.split(jax.random.fold_in(key, 31), 2)
    query_drawn = jnp.clip(jax.random.normal(first, shape, jnp.float32), -6.0, 6.0)
    key_drawn = jnp.clip(jax.random.normal(second, shape, jnp.float32), -6.0, 6.0)
    return (query_drawn, key_drawn)


def draw_queries(key, part):
    return draw_pair(key)[0].astype(jnp.bfloat16)


def draw_keys(key, part):
    return draw_pair(key)[1].astype(jnp.bfloat16)


def block_scale(key, shape, cuts, smallest, top_value):
    def one(dim, blocks):
        draws = jax.random.uniform(jax.random.fold_in(jax.random.fold_in(key, 6), dim), (blocks,), jnp.float32, smallest / len(cuts), top_value / len(cuts))
        return jnp.repeat(jnp.exp(draws), shape[dim] // blocks).reshape((-1,) + (1,) * (len(shape) - dim - 1))

    level = one(*cuts[0])
    for cut in cuts[1:]:
        level = level * one(*cut)
    return level


def length_profile(amount, total, bound, slope):
    portions = [(1 << 20) // math.isqrt(rank ** slope) + 1 for rank in range(2, amount + 1)]
    spare, counts = total - bound - (amount - 1), [1] * (amount - 1)
    while spare > 0:
        candidates = [i for i in range(amount - 1) if counts[i] < bound]
        mass, left = sum([portions[i] for i in candidates]), spare
        for i in candidates:
            addition = min(bound - counts[i], max(1, left * portions[i] // mass), spare)
            counts[i] = counts[i] + addition
            spare = spare - addition
    return np.array([bound] + counts)


def uneven_parts(own_key, count, total, limit, skew):
    if count == 2:
        one = jax.random.randint(own_key, (), max(1, total - limit), min(limit, total - 1) + 1)
        return jnp.stack([one, total - one])
    lengths = jnp.asarray(length_profile(count, total, limit, skew), jnp.int32)
    pairs = (count - 1) // 2
    source_of, taker = lengths[1:1 + 2 * pairs:2], lengths[2:2 + 2 * pairs:2]
    margin = jnp.minimum(source_of - 1, limit - taker)
    moved = jax.random.randint(jax.random.fold_in(own_key, 1), (pairs,), 0, 1 << 20) % (margin + 1)
    lengths = lengths.at[1:1 + 2 * pairs:2].set(source_of - moved).at[2:2 + 2 * pairs:2].set(taker + moved)
    return lengths[jax.random.permutation(jax.random.fold_in(own_key, 2), count)]


def bell_draw(own_key, extent, deviation, limit, cuts=(), kind=jnp.bfloat16):
    result = deviation * jax.random.normal(own_key, extent, jnp.float32)
    if cuts:
        result = result * block_scale(own_key, extent, cuts, -0.22, 0.18)
    return jnp.clip(result, -limit, limit).astype(kind)


def setup_inputs(seed: int = 0) -> dict:
    key_of = jax.random.split(jax.random.key(seed), 7)
    queries = draw_queries(jax.random.fold_in(key_of[6], 71), 0)
    keys = draw_keys(jax.random.fold_in(key_of[6], 71), 0)
    values = bell_draw(key_of[2], (SEQ, HEADS, DH), 1.0, 6.0, ((0, 64), (1, 4)))
    gain = jnp.clip(1.0 + 0.18 * jax.random.normal(key_of[3], (HEADS, DH), jnp.float32), 0.1, 1.9)
    doc_lengths = uneven_parts(key_of[4], NDOCS, SEQ, MAXDOC, 2).astype(jnp.int32)
    cotangent = bell_draw(key_of[5], (SEQ, HEADS, DH), 1.0, 6.0, ((0, 64), (1, 4)))
    return dict(queries=queries, keys=keys, values=values, gain=gain, doc_lengths=doc_lengths, cotangent=cotangent)


neg_large = -1e+30
norm_eps = 1e-06

def wide(form, left, right):
    return jnp.einsum(form, left, right, precision=lax.Precision.HIGHEST)

def doc_index(doc_lengths, positions):
    starts = jnp.cumsum(doc_lengths) - doc_lengths
    return lax.optimization_barrier(jnp.sum((starts[None, :] <= positions[:, None]).astype(jnp.int32), axis=1)) - 1

def one_doc(doc_lengths, position):
    return doc_index(doc_lengths, jnp.reshape(position, (1,)).astype(jnp.int32))[0]

def settle(array):
    return lax.optimization_barrier(array.astype(jnp.bfloat16)).astype(jnp.float32)

def reference(queries, keys, values, gain, doc_lengths, cotangent):
    tile = TOK_DEV
    count = SEQ // tile
    reach = SPAN * tile
    scale = DH ** (-0.5)
    features = HEADS * DH
    offsets = jnp.arange(tile, dtype=jnp.int32)
    spread = jnp.arange(reach + tile, dtype=jnp.int32)
    causal = (offsets[:, None] >= offsets[None, :]).astype(jnp.float32)
    indices = jnp.arange(count, dtype=jnp.int32)
    zero_state = jnp.zeros((HEADS, DH, DH), jnp.float32)
    front = jnp.zeros((reach, HEADS, DH), jnp.bfloat16)
    key_pad = jnp.concatenate([front, keys], axis=0)
    value_pad = jnp.concatenate([front, values], axis=0)
    query_pad = jnp.concatenate([queries, front], axis=0)
    grad_pad = jnp.concatenate([cotangent, front], axis=0)

    def rows(array, start, size):
        return lax.dynamic_slice_in_dim(array, start, size, 0).astype(jnp.float32)

    def back_mask(start):
        query_pos = start + offsets
        key_pos = start - reach + spread
        same = doc_index(doc_lengths, query_pos)[:, None] == doc_index(doc_lengths, key_pos)[None, :]
        return same & (key_pos[None, :] <= query_pos[:, None])

    def scores_of(query_block, key_block, mask):
        raw = wide('thd,uhd->htu', query_block, key_block) * scale
        return jnp.where(mask[None], raw, neg_large)

    def tile_info(start):
        tile_doc = doc_index(doc_lengths, start + offsets)
        same = (tile_doc[:, None] == tile_doc[None, :]).astype(jnp.float32) * causal
        prev_doc = one_doc(doc_lengths, start - 1)
        next_doc = one_doc(doc_lengths, start + tile)
        return (tile_doc, same, prev_doc, next_doc)

    def forward(state, index):
        start = index * tile
        query_tile = rows(queries, start, tile)
        key_tile = rows(keys, start, tile)
        value_tile = rows(values, start, tile)
        tile_doc, same, prev_doc, next_doc = tile_info(start)
        carried = (tile_doc == prev_doc).astype(jnp.float32)
        attend = settle(wide('thd,uhd->htu', query_tile, key_tile) * same)
        linear_tile = wide('htu,uhd->thd', attend, value_tile) + wide('thd,hde->the', query_tile, state) * carried[:, None, None]
        scores = scores_of(query_tile, rows(key_pad, start, reach + tile), back_mask(start))
        top = lax.optimization_barrier(jnp.max(scores, axis=-1))
        log_total = top + jnp.log(lax.optimization_barrier(jnp.sum(jnp.exp(scores - top[..., None]), axis=-1)))
        weights = settle(jnp.exp(scores - log_total[..., None]))
        soft_tile = wide('htu,uhd->thd', weights, rows(value_pad, start, reach + tile))
        keep = (tile_doc == tile_doc[tile - 1]).astype(jnp.float32)
        stay = (prev_doc == tile_doc[tile - 1]).astype(jnp.float32)
        new_state = state * stay + wide('uhd,uhe->hde', key_tile * keep[:, None, None], value_tile)
        return (new_state, (linear_tile, soft_tile, log_total))
    final, (linear_out, soft_out, log_total) = lax.scan(forward, zero_state, indices)
    linear_out = linear_out.reshape(SEQ, HEADS, DH)
    soft_out = soft_out.reshape(SEQ, HEADS, DH)
    inverse = lax.rsqrt(lax.optimization_barrier(jnp.sum(linear_out * linear_out, axis=(1, 2))) / features + norm_eps)
    gain_wide = gain.astype(jnp.float32)
    mixed = (linear_out * inverse[:, None, None] * gain_wide[None] + soft_out).astype(jnp.bfloat16)
    grad = cotangent.astype(jnp.float32)
    weighted = grad * gain_wide[None]
    projection = lax.optimization_barrier(jnp.sum(weighted * linear_out, axis=(1, 2)))
    inner = settle(inverse[:, None, None] * weighted - linear_out * (inverse ** 3 * projection / features)[:, None, None])
    row_dot = lax.optimization_barrier(jnp.sum(grad * soft_out, axis=-1))
    dot_tiles = jnp.transpose(row_dot.reshape(count, tile, HEADS), (0, 2, 1))

    def query_side(state, inputs):
        index, lse_tile, dot_tile = inputs
        start = index * tile
        query_tile = rows(queries, start, tile)
        key_tile = rows(keys, start, tile)
        value_tile = rows(values, start, tile)
        inner_tile = lax.dynamic_slice_in_dim(inner, start, tile, 0)
        grad_tile = rows(cotangent, start, tile)
        key_window = rows(key_pad, start, reach + tile)
        value_window = rows(value_pad, start, reach + tile)
        tile_doc, same, prev_doc, next_doc = tile_info(start)
        carried = (tile_doc == prev_doc).astype(jnp.float32)
        back = settle(wide('thd,uhd->htu', inner_tile, value_tile) * same)
        linear_grad = wide('htu,uhd->thd', back, key_tile) + wide('the,hde->thd', inner_tile, state) * carried[:, None, None]
        scores = scores_of(query_tile, key_window, back_mask(start))
        probs = jnp.exp(scores - lse_tile[..., None])
        dprobs = wide('thd,uhd->htu', grad_tile, value_window)
        dscores = settle(probs * (dprobs - dot_tile[..., None]))
        soft_grad = wide('htu,uhd->thd', dscores, key_window) * scale
        keep = (tile_doc == tile_doc[tile - 1]).astype(jnp.float32)
        stay = (prev_doc == tile_doc[tile - 1]).astype(jnp.float32)
        new_state = state * stay + wide('uhd,uhe->hde', key_tile * keep[:, None, None], value_tile)
        return (new_state, linear_grad + soft_grad)
    final, query_grad = lax.scan(query_side, zero_state, (indices, log_total, dot_tiles))
    query_grad = query_grad.reshape(SEQ, HEADS, DH).astype(jnp.bfloat16)
    tail = jnp.zeros((reach, HEADS), jnp.float32)
    lse_rows = jnp.transpose(log_total, (0, 2, 1)).reshape(SEQ, HEADS)
    lse_pad = jnp.concatenate([lse_rows, tail], axis=0)
    dot_pad = jnp.concatenate([row_dot, tail], axis=0)

    def key_side(later, index):
        start = index * tile
        query_tile = rows(queries, start, tile)
        key_tile = rows(keys, start, tile)
        value_tile = rows(values, start, tile)
        inner_tile = lax.dynamic_slice_in_dim(inner, start, tile, 0)
        tile_doc, same, prev_doc, next_doc = tile_info(start)
        carried = (tile_doc == next_doc).astype(jnp.float32)
        attend = settle(wide('thd,uhd->htu', query_tile, key_tile) * same)
        back = settle(wide('thd,uhd->htu', inner_tile, value_tile) * same)
        key_linear = wide('htu,thd->uhd', back, query_tile) + wide('uhe,hde->uhd', value_tile, later) * carried[:, None, None]
        value_linear = wide('htu,the->uhe', attend, inner_tile) + wide('uhd,hde->uhe', key_tile, later) * carried[:, None, None]
        query_pos = start + spread
        key_pos = start + offsets
        same_doc = doc_index(doc_lengths, query_pos)[:, None] == doc_index(doc_lengths, key_pos)[None, :]
        mask = same_doc & (key_pos[None, :] <= query_pos[:, None]) & (query_pos[:, None] < SEQ)
        query_window = rows(query_pad, start, reach + tile)
        grad_window = rows(grad_pad, start, reach + tile)
        lse_window = lax.dynamic_slice_in_dim(lse_pad, start, reach + tile, 0).T
        dot_window = lax.dynamic_slice_in_dim(dot_pad, start, reach + tile, 0).T
        scores = scores_of(query_window, key_tile, mask)
        probs = jnp.exp(scores - lse_window[..., None])
        weights = settle(probs)
        dprobs = wide('thd,uhd->htu', grad_window, value_tile)
        dscores = settle(probs * (dprobs - dot_window[..., None]))
        key_soft = wide('htu,thd->uhd', dscores, query_window) * scale
        value_soft = wide('htu,thd->uhd', weights, grad_window)
        keep = (tile_doc == tile_doc[0]).astype(jnp.float32)
        stay = (next_doc == tile_doc[0]).astype(jnp.float32)
        new_later = later * stay + wide('thd,the->hde', query_tile * keep[:, None, None], inner_tile)
        return (new_later, (key_linear + key_soft, value_linear + value_soft))
    final, (key_grad, value_grad) = lax.scan(key_side, zero_state, indices, reverse=True)
    key_grad = key_grad.reshape(SEQ, HEADS, DH).astype(jnp.bfloat16)
    value_grad = value_grad.reshape(SEQ, HEADS, DH).astype(jnp.bfloat16)
    return (mixed, query_grad, key_grad, value_grad)
```

```python
import jax
import jax.numpy as jnp
from jax import lax
from jax.sharding import PartitionSpec as P

SPAN = 2
MAXDOC = 2048


neg_large = -1e30
norm_eps = 1e-06


def from_behind(x, axis, by):
    devices = lax.axis_size(axis)
    pairs = [(i, i + by) for i in range(devices) if 0 <= i + by < devices]
    return lax.ppermute(x, axis, pairs)


def tile_state(keys_t, values_t, doc_lengths, start):
    tile = keys_t.shape[0]
    docs = doc_index(doc_lengths, start + jnp.arange(tile, dtype=jnp.int32))
    keep = (docs == docs[tile - 1])[:, None, None]
    state = narrow("uhd,uhe->hde", jnp.where(keep, keys_t, jnp.zeros_like(keys_t)), values_t)
    flag = (one_doc(doc_lengths, start - 1) != docs[tile - 1]).astype(jnp.float32)
    return (state, flag)


def scan_from_window(window, covered, need, axis):
    while covered < need:
        window = join_states(from_behind(window, axis, covered), window)
        covered *= 2
    return window


def suffix_scan(part, need, axis):
    covered = 1
    while 2 * covered < need:
        part = join_states(from_behind(part, axis, -covered), part)
        covered *= 2
    near = from_behind(part, axis, -1)
    if covered >= need:
        return near
    return join_states(from_behind(part, axis, -1 - covered), near)


def wide(form, left, right):
    return jnp.einsum(form, left, right, precision=lax.Precision.HIGHEST)


def narrow(form, left, right):
    return jnp.einsum(form, left, right, preferred_element_type=jnp.float32)


def doc_index(doc_lengths, positions):
    starts = jnp.cumsum(doc_lengths) - doc_lengths
    return jnp.sum((starts[None, :] <= positions[:, None]).astype(jnp.int32), axis=1) - 1


def one_doc(doc_lengths, position):
    return doc_index(doc_lengths, jnp.reshape(position, (1,)))[0]


def join_states(earlier, later):
    return (later[0] + (1.0 - later[1]) * earlier[0], jnp.maximum(earlier[1], later[1]))


def masked_scores(query_block, key_block, mask, scale):
    raw = narrow("thd,uhd->htu", query_block, key_block) * scale
    return jnp.where(mask[None], raw, neg_large)


def key_terms(dscores, weights, query_block, grad_block, scale):
    key_part = narrow("htu,thd->uhd", dscores, query_block) * scale
    value_part = narrow("htu,thd->uhd", weights, grad_block)
    return (key_part, value_part)


def per_device(queries, keys, values, gain, doc_lengths, cotangent):
    tile, heads, width = queries.shape
    features = heads * lax.axis_size("head") * width
    scale = width ** (-0.5)
    base = lax.axis_index("ctx") * tile
    offsets = jnp.arange(tile, dtype=jnp.int32)
    own_pos = base + offsets
    own_doc = doc_index(doc_lengths, own_pos)
    prev_doc = one_doc(doc_lengths, base - 1)
    next_doc = one_doc(doc_lengths, base + tile)
    pair = jnp.stack([keys, values])
    arrived = [from_behind(pair, "ctx", shift) for shift in range(SPAN, 0, -1)]
    key_tiles = [piece[0] for piece in arrived] + [keys]
    value_tiles = [piece[1] for piece in arrived] + [values]
    masks = []
    for position in range(SPAN + 1):
        key_pos = base - (SPAN - position) * tile + offsets
        key_doc = doc_index(doc_lengths, key_pos)
        masks.append(
            (own_doc[:, None] == key_doc[None, :]) & (key_pos[None, :] <= own_pos[:, None])
        )
    score_list = [
        masked_scores(queries, key_tiles[position], masks[position], scale)
        for position in range(SPAN + 1)
    ]
    top = score_list[0].max(axis=-1)
    for position in range(1, SPAN + 1):
        top = jnp.maximum(top, score_list[position].max(axis=-1))
    total = jnp.zeros((heads, tile), jnp.float32)
    for position in range(SPAN + 1):
        total = total + jnp.sum(jnp.exp(score_list[position] - top[..., None]), axis=-1)
    log_total = top + jnp.log(total)
    prob_list = []
    weight_list = []
    soft_out = jnp.zeros((tile, heads, width), jnp.float32)
    for position in range(SPAN + 1):
        probs = jnp.exp(score_list[position] - log_total[..., None])
        weights = probs.astype(jnp.bfloat16)
        prob_list.append(probs)
        weight_list.append(weights)
        soft_out = soft_out + narrow("htu,uhd->thd", weights, value_tiles[position])
    same_tile = masks[SPAN].astype(jnp.float32)
    carried_prev = (own_doc == prev_doc).astype(jnp.float32)
    carried_next = (own_doc == next_doc).astype(jnp.float32)
    keep_first = (own_doc == own_doc[0])[:, None, None]
    reset_back = (next_doc != own_doc[0]).astype(jnp.float32)
    query_wide = queries.astype(jnp.float32)
    attend = (narrow("thd,uhd->htu", queries, keys) * same_tile).astype(jnp.bfloat16)
    need = min(-(-MAXDOC // tile), lax.axis_size("ctx"))
    window = tile_state(key_tiles[0], value_tiles[0], doc_lengths, base - SPAN * tile)
    for position in range(1, SPAN):
        window = join_states(
            window,
            tile_state(
                key_tiles[position], value_tiles[position], doc_lengths,
                base - (SPAN - position) * tile,
            ),
        )
    incoming, front_flag = scan_from_window(window, SPAN, need, "ctx")
    linear_out = (
        narrow("htu,uhd->thd", attend, values)
        + wide("thd,hde->the", query_wide, incoming) * carried_prev[:, None, None]
    )
    squares = lax.psum(jnp.sum(linear_out * linear_out, axis=(1, 2)), "head")
    inverse = lax.rsqrt(squares / features + norm_eps)
    mixed = (linear_out * inverse[:, None, None] * gain[None] + soft_out).astype(jnp.bfloat16)
    grad_wide = cotangent.astype(jnp.float32)
    weighted = grad_wide * gain[None]
    projection = lax.psum(jnp.sum(weighted * linear_out, axis=(1, 2)), "head")
    inner = (
        inverse[:, None, None] * weighted
        - linear_out * (inverse**3 * projection / features)[:, None, None]
    ).astype(jnp.bfloat16)
    row_dot = jnp.sum(grad_wide * soft_out, axis=-1).T
    query_soft = jnp.zeros((tile, heads, width), jnp.float32)
    dscore_list = []
    for position in range(SPAN + 1):
        dprobs = narrow("thd,uhd->htu", cotangent, value_tiles[position])
        dscores = (prob_list[position] * (dprobs - row_dot[..., None])).astype(jnp.bfloat16)
        query_soft = query_soft + narrow("htu,uhd->thd", dscores, key_tiles[position]) * scale
        dscore_list.append(dscores)
    inner_wide = inner.astype(jnp.float32)
    back = (narrow("thd,uhd->htu", inner, values) * same_tile).astype(jnp.bfloat16)
    query_linear = (
        narrow("htu,uhd->thd", back, keys)
        + wide("the,hde->thd", inner_wide, incoming) * carried_prev[:, None, None]
    )
    tile_sum = narrow(
        "thd,the->hde", jnp.where(keep_first, queries, jnp.zeros_like(queries)), inner
    )
    later, back_flag = suffix_scan((tile_sum, reset_back), need, "ctx")
    key_linear = (
        narrow("htu,thd->uhd", back, queries)
        + wide("uhe,hde->uhd", values.astype(jnp.float32), later) * carried_next[:, None, None]
    )
    value_linear = (
        narrow("htu,the->uhe", attend, inner)
        + wide("uhd,hde->uhe", keys.astype(jnp.float32), later) * carried_next[:, None, None]
    )
    parts = [
        key_terms(dscore_list[position], weight_list[position], queries, cotangent, scale)
        for position in range(SPAN + 1)
    ]
    key_soft, value_soft = parts[SPAN]
    for shift in range(1, SPAN + 1):
        sent = jnp.stack([parts[SPAN - shift][0], parts[SPAN - shift][1]])
        returned = from_behind(sent.astype(jnp.bfloat16), "ctx", -shift).astype(sent.dtype)
        key_soft = key_soft + returned[0]
        value_soft = value_soft + returned[1]
    query_grad = (query_linear + query_soft).astype(jnp.bfloat16)
    key_grad = (key_linear + key_soft).astype(jnp.bfloat16)
    value_grad = (value_linear + value_soft).astype(jnp.bfloat16)
    return (mixed, query_grad, key_grad, value_grad)


def solution(mesh):
    placed = (
        P("ctx", "head", None),
        P("ctx", "head", None),
        P("ctx", "head", None),
        P("head", None),
        P(),
        P("ctx", "head", None),
    )
    return jax.shard_map(
        per_device,
        mesh=mesh,
        in_specs=placed,
        out_specs=(
            P("ctx", "head", None),
            P("ctx", "head", None),
            P("ctx", "head", None),
            P("ctx", "head", None),
        ),
        check_vma=False,
    )
```

```python
import jax
import jax.numpy as jnp
from jax import lax
from jax.sharding import PartitionSpec as P

SPAN = 2
MAXDOC = 2048


neg_large = -1e30
norm_eps = 1e-06


def from_behind(x, axis, by):
    devices = lax.axis_size(axis)
    pairs = [(i, i + by) for i in range(devices) if 0 <= i + by < devices]
    return lax.ppermute(x, axis, pairs)


def tile_state(keys_t, values_t, doc_lengths, start):
    tile = keys_t.shape[0]
    docs = doc_index(doc_lengths, start + jnp.arange(tile, dtype=jnp.int32))
    keep = (docs == docs[tile - 1])[:, None, None]
    return narrow("uhd,uhe->hde", jnp.where(keep, keys_t, jnp.zeros_like(keys_t)), values_t)


def fold_states(pieces, flags):
    total = pieces[0]
    for piece, flag in zip(pieces[1:], flags[1:]):
        total = piece + (1.0 - flag) * total
    return total


def front_flags(doc_lengths, spans, tile):
    low = jnp.stack([lo * tile - 1 for lo, hi in spans])
    high = jnp.stack([hi * tile + tile - 1 for lo, hi in spans])
    docs = doc_index(doc_lengths, jnp.concatenate([low, high]).astype(jnp.int32))
    count = len(spans)
    return (docs[:count] != docs[count:]).astype(jnp.float32)


def back_flags(doc_lengths, spans, tile):
    low = jnp.stack([lo * tile for lo, hi in spans])
    high = jnp.stack([hi * tile + tile for lo, hi in spans])
    docs = doc_index(doc_lengths, jnp.concatenate([low, high]).astype(jnp.int32))
    count = len(spans)
    return (docs[:count] != docs[count:]).astype(jnp.float32)


def wide(form, left, right):
    return jnp.einsum(form, left, right, precision=lax.Precision.HIGHEST)


def narrow(form, left, right):
    return jnp.einsum(form, left, right, preferred_element_type=jnp.float32)


def doc_index(doc_lengths, positions):
    starts = jnp.cumsum(doc_lengths) - doc_lengths
    return jnp.sum((starts[None, :] <= positions[:, None]).astype(jnp.int32), axis=1) - 1


def one_doc(doc_lengths, position):
    return doc_index(doc_lengths, jnp.reshape(position, (1,)))[0]


def masked_scores(query_block, key_block, mask, scale):
    raw = narrow("thd,uhd->htu", query_block, key_block) * scale
    return jnp.where(mask[None], raw, neg_large)


def key_terms(dscores, weights, query_block, grad_block, scale):
    key_part = narrow("htu,thd->uhd", dscores, query_block) * scale
    value_part = narrow("htu,thd->uhd", weights, grad_block)
    return (key_part, value_part)


def per_device(queries, keys, values, gain, doc_lengths, cotangent):
    tile, heads, width = queries.shape
    features = heads * lax.axis_size("head") * width
    scale = width ** (-0.5)
    base = lax.axis_index("ctx") * tile
    offsets = jnp.arange(tile, dtype=jnp.int32)
    own_pos = base + offsets
    own_doc = doc_index(doc_lengths, own_pos)
    prev_doc = one_doc(doc_lengths, base - 1)
    next_doc = one_doc(doc_lengths, base + tile)
    pair = jnp.stack([keys, values])
    arrived = [from_behind(pair, "ctx", shift) for shift in range(SPAN, 0, -1)]
    key_tiles = [piece[0] for piece in arrived] + [keys]
    value_tiles = [piece[1] for piece in arrived] + [values]
    masks = []
    for position in range(SPAN + 1):
        key_pos = base - (SPAN - position) * tile + offsets
        key_doc = doc_index(doc_lengths, key_pos)
        masks.append(
            (own_doc[:, None] == key_doc[None, :]) & (key_pos[None, :] <= own_pos[:, None])
        )
    score_list = [
        masked_scores(queries, key_tiles[position], masks[position], scale)
        for position in range(SPAN + 1)
    ]
    top = score_list[0].max(axis=-1)
    for position in range(1, SPAN + 1):
        top = jnp.maximum(top, score_list[position].max(axis=-1))
    total = jnp.zeros((heads, tile), jnp.float32)
    for position in range(SPAN + 1):
        total = total + jnp.sum(jnp.exp(score_list[position] - top[..., None]), axis=-1)
    log_total = top + jnp.log(total)
    prob_list = []
    weight_list = []
    soft_out = jnp.zeros((tile, heads, width), jnp.float32)
    for position in range(SPAN + 1):
        probs = jnp.exp(score_list[position] - log_total[..., None])
        weights = probs.astype(jnp.bfloat16)
        prob_list.append(probs)
        weight_list.append(weights)
        soft_out = soft_out + narrow("htu,uhd->thd", weights, value_tiles[position])
    same_tile = masks[SPAN].astype(jnp.float32)
    carried_prev = (own_doc == prev_doc).astype(jnp.float32)
    carried_next = (own_doc == next_doc).astype(jnp.float32)
    keep_first = (own_doc == own_doc[0])[:, None, None]
    query_wide = queries.astype(jnp.float32)
    attend = (narrow("thd,uhd->htu", queries, keys) * same_tile).astype(jnp.bfloat16)
    place = lax.axis_index("ctx")
    need = min(-(-MAXDOC // tile), lax.axis_size("ctx"))
    group = SPAN + 2
    rounds = -(-need // group)
    own_state = tile_state(keys, values, doc_lengths, base)
    far_states = [
        from_behind(own_state, "ctx", shift) for shift in range(group - 1, SPAN, -1)
    ]
    near_states = [
        tile_state(key_tiles[position], value_tiles[position], doc_lengths,
                   base - (SPAN - position) * tile)
        for position in range(SPAN)
    ]
    group_spans = [(place - shift, place - shift) for shift in range(group - 1, -1, -1)]
    group_state = fold_states(
        far_states + near_states + [own_state], front_flags(doc_lengths, group_spans, tile)
    )
    shifts = [1 + group * k for k in range(rounds - 1, -1, -1)]
    window_spans = [(place - shift - group + 1, place - shift) for shift in shifts]
    incoming = fold_states(
        [from_behind(group_state, "ctx", shift) for shift in shifts],
        front_flags(doc_lengths, window_spans, tile),
    )
    linear_out = (
        narrow("htu,uhd->thd", attend, values)
        + wide("thd,hde->the", query_wide, incoming) * carried_prev[:, None, None]
    )
    squares = lax.psum(jnp.sum(linear_out * linear_out, axis=(1, 2)), "head")
    inverse = lax.rsqrt(squares / features + norm_eps)
    mixed = (linear_out * inverse[:, None, None] * gain[None] + soft_out).astype(jnp.bfloat16)
    grad_wide = cotangent.astype(jnp.float32)
    weighted = grad_wide * gain[None]
    projection = lax.psum(jnp.sum(weighted * linear_out, axis=(1, 2)), "head")
    inner = (
        inverse[:, None, None] * weighted
        - linear_out * (inverse**3 * projection / features)[:, None, None]
    ).astype(jnp.bfloat16)
    row_dot = jnp.sum(grad_wide * soft_out, axis=-1).T
    query_soft = jnp.zeros((tile, heads, width), jnp.float32)
    dscore_list = []
    for position in range(SPAN + 1):
        dprobs = narrow("thd,uhd->htu", cotangent, value_tiles[position])
        dscores = (prob_list[position] * (dprobs - row_dot[..., None])).astype(jnp.bfloat16)
        query_soft = query_soft + narrow("htu,uhd->thd", dscores, key_tiles[position]) * scale
        dscore_list.append(dscores)
    inner_wide = inner.astype(jnp.float32)
    back = (narrow("thd,uhd->htu", inner, values) * same_tile).astype(jnp.bfloat16)
    query_linear = (
        narrow("htu,uhd->thd", back, keys)
        + wide("the,hde->thd", inner_wide, incoming) * carried_prev[:, None, None]
    )
    tile_sum = narrow(
        "thd,the->hde", jnp.where(keep_first, queries, jnp.zeros_like(queries)), inner
    )
    back_states = [
        from_behind(tile_sum, "ctx", -shift) for shift in range(group - 1, 0, -1)
    ] + [tile_sum]
    back_spans = [(place + shift, place + shift) for shift in range(group - 1, -1, -1)]
    back_group = fold_states(back_states, back_flags(doc_lengths, back_spans, tile))
    back_window = [(place + shift, place + shift + group - 1) for shift in shifts]
    later = fold_states(
        [from_behind(back_group, "ctx", -shift) for shift in shifts],
        back_flags(doc_lengths, back_window, tile),
    )
    key_linear = (
        narrow("htu,thd->uhd", back, queries)
        + wide("uhe,hde->uhd", values.astype(jnp.float32), later) * carried_next[:, None, None]
    )
    value_linear = (
        narrow("htu,the->uhe", attend, inner)
        + wide("uhd,hde->uhe", keys.astype(jnp.float32), later) * carried_next[:, None, None]
    )
    parts = [
        key_terms(dscore_list[position], weight_list[position], queries, cotangent, scale)
        for position in range(SPAN + 1)
    ]
    key_soft, value_soft = parts[SPAN]
    for shift in range(1, SPAN + 1):
        sent = jnp.stack([parts[SPAN - shift][0], parts[SPAN - shift][1]])
        returned = from_behind(sent.astype(jnp.bfloat16), "ctx", -shift).astype(sent.dtype)
        key_soft = key_soft + returned[0]
        value_soft = value_soft + returned[1]
    query_grad = (query_linear + query_soft).astype(jnp.bfloat16)
    key_grad = (key_linear + key_soft).astype(jnp.bfloat16)
    value_grad = (value_linear + value_soft).astype(jnp.bfloat16)
    return (mixed, query_grad, key_grad, value_grad)


def solution(mesh):
    placed = (
        P("ctx", "head", None),
        P("ctx", "head", None),
        P("ctx", "head", None),
        P("head", None),
        P(),
        P("ctx", "head", None),
    )
    return jax.shard_map(
        per_device,
        mesh=mesh,
        in_specs=placed,
        out_specs=(
            P("ctx", "head", None),
            P("ctx", "head", None),
            P("ctx", "head", None),
            P("ctx", "head", None),
        ),
        check_vma=False,
    )
```

```python
import jax
import jax.numpy as jnp
from jax import lax
from jax.sharding import PartitionSpec as P

SPAN = 2
MAXDOC = 2048


neg_large = -1e30
norm_eps = 1e-06


def from_behind(x, axis, by):
    devices = lax.axis_size(axis)
    pairs = [(i, i + by) for i in range(devices) if 0 <= i + by < devices]
    return lax.ppermute(x, axis, pairs)


def tile_state(keys_t, values_t, doc_lengths, start):
    tile = keys_t.shape[0]
    docs = doc_index(doc_lengths, start + jnp.arange(tile, dtype=jnp.int32))
    keep = (docs == docs[tile - 1])[:, None, None]
    return narrow("uhd,uhe->hde", jnp.where(keep, keys_t, jnp.zeros_like(keys_t)), values_t)


def fold_states(pieces, flags):
    total = pieces[0]
    for piece, flag in zip(pieces[1:], flags[1:]):
        total = piece + (1.0 - flag) * total
    return total


def front_flags(doc_lengths, spans, tile):
    low = jnp.stack([lo * tile - 1 for lo, hi in spans])
    high = jnp.stack([hi * tile + tile - 1 for lo, hi in spans])
    docs = doc_index(doc_lengths, jnp.concatenate([low, high]).astype(jnp.int32))
    count = len(spans)
    return (docs[:count] != docs[count:]).astype(jnp.float32)


def back_flags(doc_lengths, spans, tile):
    low = jnp.stack([lo * tile for lo, hi in spans])
    high = jnp.stack([hi * tile + tile for lo, hi in spans])
    docs = doc_index(doc_lengths, jnp.concatenate([low, high]).astype(jnp.int32))
    count = len(spans)
    return (docs[:count] != docs[count:]).astype(jnp.float32)


def wide(form, left, right):
    return jnp.einsum(form, left, right, precision=lax.Precision.HIGHEST)


def narrow(form, left, right):
    return jnp.einsum(form, left, right, preferred_element_type=jnp.float32)


def doc_index(doc_lengths, positions):
    starts = jnp.cumsum(doc_lengths) - doc_lengths
    return jnp.sum((starts[None, :] <= positions[:, None]).astype(jnp.int32), axis=1) - 1


def one_doc(doc_lengths, position):
    return doc_index(doc_lengths, jnp.reshape(position, (1,)))[0]


def masked_scores(query_block, key_block, mask, scale):
    raw = narrow("thd,uhd->htu", query_block, key_block) * scale
    return jnp.where(mask[None], raw, neg_large)


def key_terms(dscores, weights, query_block, grad_block, scale):
    key_part = narrow("htu,thd->uhd", dscores, query_block) * scale
    value_part = narrow("htu,thd->uhd", weights, grad_block)
    return (key_part, value_part)


def per_device(queries, keys, values, gain, doc_lengths, cotangent):
    tile, heads, width = queries.shape
    features = heads * lax.axis_size("head") * width
    scale = width ** (-0.5)
    base = lax.axis_index("ctx") * tile
    offsets = jnp.arange(tile, dtype=jnp.int32)
    own_pos = base + offsets
    own_doc = doc_index(doc_lengths, own_pos)
    prev_doc = one_doc(doc_lengths, base - 1)
    next_doc = one_doc(doc_lengths, base + tile)
    pair = jnp.stack([keys, values])
    arrived = [from_behind(pair, "ctx", shift) for shift in range(SPAN, 0, -1)]
    key_tiles = [piece[0] for piece in arrived] + [keys]
    value_tiles = [piece[1] for piece in arrived] + [values]
    masks = []
    for position in range(SPAN + 1):
        key_pos = base - (SPAN - position) * tile + offsets
        key_doc = doc_index(doc_lengths, key_pos)
        masks.append(
            (own_doc[:, None] == key_doc[None, :]) & (key_pos[None, :] <= own_pos[:, None])
        )
    score_list = [
        masked_scores(queries, key_tiles[position], masks[position], scale)
        for position in range(SPAN + 1)
    ]
    top = score_list[0].max(axis=-1)
    for position in range(1, SPAN + 1):
        top = jnp.maximum(top, score_list[position].max(axis=-1))
    total = jnp.zeros((heads, tile), jnp.float32)
    for position in range(SPAN + 1):
        total = total + jnp.sum(jnp.exp(score_list[position] - top[..., None]), axis=-1)
    log_total = top + jnp.log(total)
    prob_list = []
    weight_list = []
    soft_out = jnp.zeros((tile, heads, width), jnp.float32)
    for position in range(SPAN + 1):
        probs = jnp.exp(score_list[position] - log_total[..., None])
        weights = probs.astype(jnp.bfloat16)
        prob_list.append(probs)
        weight_list.append(weights)
        soft_out = soft_out + narrow("htu,uhd->thd", weights, value_tiles[position])
    same_tile = masks[SPAN].astype(jnp.float32)
    carried_prev = (own_doc == prev_doc).astype(jnp.float32)
    carried_next = (own_doc == next_doc).astype(jnp.float32)
    keep_first = (own_doc == own_doc[0])[:, None, None]
    query_wide = queries.astype(jnp.float32)
    attend = (narrow("thd,uhd->htu", queries, keys) * same_tile).astype(jnp.bfloat16)
    place = lax.axis_index("ctx")
    need = min(-(-MAXDOC // tile), lax.axis_size("ctx"))
    near_states = [
        tile_state(key_tiles[position], value_tiles[position], doc_lengths,
                   base - (SPAN - position) * tile)
        for position in range(SPAN)
    ]
    near_spans = [(place - SPAN + position, place - SPAN + position) for position in range(SPAN)]
    incoming = fold_states(near_states, front_flags(doc_lengths, near_spans, tile))
    covered = SPAN
    while covered < need:
        (flag,) = front_flags(doc_lengths, [(place - covered, place - 1)], tile)
        incoming = incoming + (1.0 - flag) * from_behind(incoming, "ctx", covered)
        covered *= 2
    linear_out = (
        narrow("htu,uhd->thd", attend, values)
        + wide("thd,hde->the", query_wide, incoming) * carried_prev[:, None, None]
    )
    squares = lax.psum(jnp.sum(linear_out * linear_out, axis=(1, 2)), "head")
    inverse = lax.rsqrt(squares / features + norm_eps)
    mixed = (linear_out * inverse[:, None, None] * gain[None] + soft_out).astype(jnp.bfloat16)
    grad_wide = cotangent.astype(jnp.float32)
    weighted = grad_wide * gain[None]
    projection = lax.psum(jnp.sum(weighted * linear_out, axis=(1, 2)), "head")
    inner = (
        inverse[:, None, None] * weighted
        - linear_out * (inverse**3 * projection / features)[:, None, None]
    ).astype(jnp.bfloat16)
    row_dot = jnp.sum(grad_wide * soft_out, axis=-1).T
    query_soft = jnp.zeros((tile, heads, width), jnp.float32)
    dscore_list = []
    for position in range(SPAN + 1):
        dprobs = narrow("thd,uhd->htu", cotangent, value_tiles[position])
        dscores = (prob_list[position] * (dprobs - row_dot[..., None])).astype(jnp.bfloat16)
        query_soft = query_soft + narrow("htu,uhd->thd", dscores, key_tiles[position]) * scale
        dscore_list.append(dscores)
    inner_wide = inner.astype(jnp.float32)
    back = (narrow("thd,uhd->htu", inner, values) * same_tile).astype(jnp.bfloat16)
    query_linear = (
        narrow("htu,uhd->thd", back, keys)
        + wide("the,hde->thd", inner_wide, incoming) * carried_prev[:, None, None]
    )
    tile_sum = narrow(
        "thd,the->hde", jnp.where(keep_first, queries, jnp.zeros_like(queries)), inner
    )
    part = tile_sum
    covered = 1
    while 2 * covered < need:
        (flag,) = back_flags(doc_lengths, [(place, place + covered - 1)], tile)
        part = part + (1.0 - flag) * from_behind(part, "ctx", -covered)
        covered *= 2
    later = from_behind(part, "ctx", -1)
    if covered < need:
        (flag,) = back_flags(doc_lengths, [(place + 1, place + covered)], tile)
        later = later + (1.0 - flag) * from_behind(part, "ctx", -1 - covered)
    key_linear = (
        narrow("htu,thd->uhd", back, queries)
        + wide("uhe,hde->uhd", values.astype(jnp.float32), later) * carried_next[:, None, None]
    )
    value_linear = (
        narrow("htu,the->uhe", attend, inner)
        + wide("uhd,hde->uhe", keys.astype(jnp.float32), later) * carried_next[:, None, None]
    )
    parts = [
        key_terms(dscore_list[position], weight_list[position], queries, cotangent, scale)
        for position in range(SPAN + 1)
    ]
    key_soft, value_soft = parts[SPAN]
    for shift in range(1, SPAN + 1):
        sent = jnp.stack([parts[SPAN - shift][0], parts[SPAN - shift][1]])
        returned = from_behind(sent.astype(jnp.bfloat16), "ctx", -shift).astype(sent.dtype)
        key_soft = key_soft + returned[0]
        value_soft = value_soft + returned[1]
    query_grad = (query_linear + query_soft).astype(jnp.bfloat16)
    key_grad = (key_linear + key_soft).astype(jnp.bfloat16)
    value_grad = (value_linear + value_soft).astype(jnp.bfloat16)
    return (mixed, query_grad, key_grad, value_grad)


def solution(mesh):
    placed = (
        P("ctx", "head", None),
        P("ctx", "head", None),
        P("ctx", "head", None),
        P("head", None),
        P(),
        P("ctx", "head", None),
    )
    return jax.shard_map(
        per_device,
        mesh=mesh,
        in_specs=placed,
        out_specs=(
            P("ctx", "head", None),
            P("ctx", "head", None),
            P("ctx", "head", None),
            P("ctx", "head", None),
        ),
        check_vma=False,
    )
```

```python
import jax
import jax.numpy as jnp
from jax import lax
from jax.sharding import PartitionSpec as P

SPAN = 2
MAXDOC = 2048


neg_large = -1e30
norm_eps = 1e-06


def from_behind(x, axis, by):
    devices = lax.axis_size(axis)
    pairs = [(i, i + by) for i in range(devices) if 0 <= i + by < devices]
    return lax.ppermute(x, axis, pairs)


def send_state(x, axis, by):
    return from_behind(x.astype(jnp.bfloat16), axis, by).astype(jnp.float32)


def send_with(state, extra, axis, by):
    width = state.shape[-1]
    flat = jnp.concatenate(
        [state.astype(jnp.bfloat16).reshape(-1, width), extra.astype(jnp.bfloat16).reshape(-1, width)]
    )
    moved = from_behind(flat, axis, by)
    cut = state.size // width
    return (
        moved[:cut].reshape(state.shape).astype(jnp.float32),
        moved[cut:].reshape(extra.shape).astype(jnp.float32),
    )


def tile_state(keys_t, values_t, doc_lengths, start):
    tile = keys_t.shape[0]
    docs = doc_index(doc_lengths, start + jnp.arange(tile, dtype=jnp.int32))
    keep = (docs == docs[tile - 1])[:, None, None]
    return narrow("uhd,uhe->hde", jnp.where(keep, keys_t, jnp.zeros_like(keys_t)), values_t)


def fold_states(pieces, flags):
    total = pieces[0]
    for piece, flag in zip(pieces[1:], flags[1:]):
        total = piece + (1.0 - flag) * total
    return total


def front_flags(doc_lengths, spans, tile):
    low = jnp.stack([lo * tile - 1 for lo, hi in spans])
    high = jnp.stack([hi * tile + tile - 1 for lo, hi in spans])
    docs = doc_index(doc_lengths, jnp.concatenate([low, high]).astype(jnp.int32))
    count = len(spans)
    return (docs[:count] != docs[count:]).astype(jnp.float32)


def back_flags(doc_lengths, spans, tile):
    low = jnp.stack([lo * tile for lo, hi in spans])
    high = jnp.stack([hi * tile + tile for lo, hi in spans])
    docs = doc_index(doc_lengths, jnp.concatenate([low, high]).astype(jnp.int32))
    count = len(spans)
    return (docs[:count] != docs[count:]).astype(jnp.float32)


def wide(form, left, right):
    return jnp.einsum(form, left, right, precision=lax.Precision.HIGHEST)


def narrow(form, left, right):
    return jnp.einsum(form, left, right, preferred_element_type=jnp.float32)


def doc_index(doc_lengths, positions):
    starts = jnp.cumsum(doc_lengths) - doc_lengths
    return jnp.sum((starts[None, :] <= positions[:, None]).astype(jnp.int32), axis=1) - 1


def one_doc(doc_lengths, position):
    return doc_index(doc_lengths, jnp.reshape(position, (1,)))[0]


def masked_scores(query_block, key_block, mask, scale):
    raw = narrow("thd,uhd->htu", query_block, key_block) * scale
    return jnp.where(mask[None], raw, neg_large)


def key_terms(dscores, weights, query_block, grad_block, scale):
    key_part = narrow("htu,thd->uhd", dscores, query_block) * scale
    value_part = narrow("htu,thd->uhd", weights, grad_block)
    return (key_part, value_part)


def per_device(queries, keys, values, gain, doc_lengths, cotangent):
    tile, heads, width = queries.shape
    features = heads * lax.axis_size("head") * width
    scale = width ** (-0.5)
    base = lax.axis_index("ctx") * tile
    offsets = jnp.arange(tile, dtype=jnp.int32)
    own_pos = base + offsets
    own_doc = doc_index(doc_lengths, own_pos)
    prev_doc = one_doc(doc_lengths, base - 1)
    next_doc = one_doc(doc_lengths, base + tile)
    pair = jnp.stack([keys, values])
    arrived = [from_behind(pair, "ctx", shift) for shift in range(SPAN, 0, -1)]
    key_tiles = [piece[0] for piece in arrived] + [keys]
    value_tiles = [piece[1] for piece in arrived] + [values]
    masks = []
    for position in range(SPAN + 1):
        key_pos = base - (SPAN - position) * tile + offsets
        key_doc = doc_index(doc_lengths, key_pos)
        masks.append(
            (own_doc[:, None] == key_doc[None, :]) & (key_pos[None, :] <= own_pos[:, None])
        )
    score_list = [
        masked_scores(queries, key_tiles[position], masks[position], scale)
        for position in range(SPAN + 1)
    ]
    top = score_list[0].max(axis=-1)
    for position in range(1, SPAN + 1):
        top = jnp.maximum(top, score_list[position].max(axis=-1))
    total = jnp.zeros((heads, tile), jnp.float32)
    for position in range(SPAN + 1):
        total = total + jnp.sum(jnp.exp(score_list[position] - top[..., None]), axis=-1)
    log_total = top + jnp.log(total)
    prob_list = []
    weight_list = []
    soft_out = jnp.zeros((tile, heads, width), jnp.float32)
    for position in range(SPAN + 1):
        probs = jnp.exp(score_list[position] - log_total[..., None])
        weights = probs.astype(jnp.bfloat16)
        prob_list.append(probs)
        weight_list.append(weights)
        soft_out = soft_out + narrow("htu,uhd->thd", weights, value_tiles[position])
    same_tile = masks[SPAN].astype(jnp.float32)
    carried_prev = (own_doc == prev_doc).astype(jnp.float32)
    carried_next = (own_doc == next_doc).astype(jnp.float32)
    keep_first = (own_doc == own_doc[0])[:, None, None]
    query_wide = queries.astype(jnp.float32)
    attend = (narrow("thd,uhd->htu", queries, keys) * same_tile).astype(jnp.bfloat16)
    place = lax.axis_index("ctx")
    need = min(-(-MAXDOC // tile), lax.axis_size("ctx"))
    near_states = [
        tile_state(key_tiles[position], value_tiles[position], doc_lengths,
                   base - (SPAN - position) * tile)
        for position in range(SPAN)
    ]
    near_spans = [(place - SPAN + position, place - SPAN + position) for position in range(SPAN)]
    incoming = fold_states(near_states, front_flags(doc_lengths, near_spans, tile))
    covered = SPAN
    while covered < need:
        (flag,) = front_flags(doc_lengths, [(place - covered, place - 1)], tile)
        incoming = incoming + (1.0 - flag) * send_state(incoming, "ctx", covered)
        covered *= 2
    linear_out = (
        narrow("htu,uhd->thd", attend, values)
        + wide("thd,hde->the", query_wide, incoming) * carried_prev[:, None, None]
    )
    squares = lax.psum(jnp.sum(linear_out * linear_out, axis=(1, 2)), "head")
    inverse = lax.rsqrt(squares / features + norm_eps)
    mixed = (linear_out * inverse[:, None, None] * gain[None] + soft_out).astype(jnp.bfloat16)
    grad_wide = cotangent.astype(jnp.float32)
    weighted = grad_wide * gain[None]
    projection = lax.psum(jnp.sum(weighted * linear_out, axis=(1, 2)), "head")
    inner = (
        inverse[:, None, None] * weighted
        - linear_out * (inverse**3 * projection / features)[:, None, None]
    ).astype(jnp.bfloat16)
    row_dot = jnp.sum(grad_wide * soft_out, axis=-1).T
    query_soft = jnp.zeros((tile, heads, width), jnp.float32)
    dscore_list = []
    for position in range(SPAN + 1):
        dprobs = narrow("thd,uhd->htu", cotangent, value_tiles[position])
        dscores = (prob_list[position] * (dprobs - row_dot[..., None])).astype(jnp.bfloat16)
        query_soft = query_soft + narrow("htu,uhd->thd", dscores, key_tiles[position]) * scale
        dscore_list.append(dscores)
    inner_wide = inner.astype(jnp.float32)
    back = (narrow("thd,uhd->htu", inner, values) * same_tile).astype(jnp.bfloat16)
    query_linear = (
        narrow("htu,uhd->thd", back, keys)
        + wide("the,hde->thd", inner_wide, incoming) * carried_prev[:, None, None]
    )
    tile_sum = narrow(
        "thd,the->hde", jnp.where(keep_first, queries, jnp.zeros_like(queries)), inner
    )
    parts = [
        key_terms(dscore_list[position], weight_list[position], queries, cotangent, scale)
        for position in range(SPAN + 1)
    ]
    key_soft, value_soft = parts[SPAN]
    pending = list(range(1, SPAN + 1))

    def returned_soft(key_soft, value_soft, moved):
        return (key_soft + moved[0], value_soft + moved[1])

    part = tile_sum
    covered = 1
    while 2 * covered < need:
        (flag,) = back_flags(doc_lengths, [(place, place + covered - 1)], tile)
        if covered in pending:
            pending.remove(covered)
            sent = jnp.stack(list(parts[SPAN - covered]))
            received, moved = send_with(part, sent, "ctx", -covered)
            key_soft, value_soft = returned_soft(key_soft, value_soft, moved)
        else:
            received = send_state(part, "ctx", -covered)
        part = part + (1.0 - flag) * received
        covered *= 2
    later = send_state(part, "ctx", -1)
    if covered < need:
        (flag,) = back_flags(doc_lengths, [(place + 1, place + covered)], tile)
        later = later + (1.0 - flag) * send_state(part, "ctx", -1 - covered)
    for shift in pending:
        sent = jnp.stack([parts[SPAN - shift][0], parts[SPAN - shift][1]])
        moved = from_behind(sent.astype(jnp.bfloat16), "ctx", -shift).astype(sent.dtype)
        key_soft, value_soft = returned_soft(key_soft, value_soft, moved)
    key_linear = (
        narrow("htu,thd->uhd", back, queries)
        + wide("uhe,hde->uhd", values.astype(jnp.float32), later) * carried_next[:, None, None]
    )
    value_linear = (
        narrow("htu,the->uhe", attend, inner)
        + wide("uhd,hde->uhe", keys.astype(jnp.float32), later) * carried_next[:, None, None]
    )
    query_grad = (query_linear + query_soft).astype(jnp.bfloat16)
    key_grad = (key_linear + key_soft).astype(jnp.bfloat16)
    value_grad = (value_linear + value_soft).astype(jnp.bfloat16)
    return (mixed, query_grad, key_grad, value_grad)


def solution(mesh):
    placed = (
        P("ctx", "head", None),
        P("ctx", "head", None),
        P("ctx", "head", None),
        P("head", None),
        P(),
        P("ctx", "head", None),
    )
    return jax.shard_map(
        per_device,
        mesh=mesh,
        in_specs=placed,
        out_specs=(
            P("ctx", "head", None),
            P("ctx", "head", None),
            P("ctx", "head", None),
            P("ctx", "head", None),
        ),
        check_vma=False,
    )
```

```python
import jax
import jax.numpy as jnp
from jax import lax
from jax.sharding import PartitionSpec as P

SPAN = 2
MAXDOC = 2048


neg_large = -1e30
norm_eps = 1e-06


def from_behind(x, axis, by):
    devices = lax.axis_size(axis)
    pairs = [(i, i + by) for i in range(devices) if 0 <= i + by < devices]
    return lax.ppermute(x, axis, pairs)


def send_state(x, axis, by):
    return from_behind(x.astype(jnp.bfloat16), axis, by).astype(jnp.float32)


def tile_state(keys_t, values_t, doc_lengths, start):
    tile = keys_t.shape[0]
    docs = doc_index(doc_lengths, start + jnp.arange(tile, dtype=jnp.int32))
    keep = (docs == docs[tile - 1])[:, None, None]
    return narrow("uhd,uhe->hde", jnp.where(keep, keys_t, jnp.zeros_like(keys_t)), values_t)


def fold_states(pieces, flags):
    total = pieces[0]
    for piece, flag in zip(pieces[1:], flags[1:]):
        total = piece + (1.0 - flag) * total
    return total


def front_flags(doc_lengths, spans, tile):
    low = jnp.stack([lo * tile - 1 for lo, hi in spans])
    high = jnp.stack([hi * tile + tile - 1 for lo, hi in spans])
    docs = doc_index(doc_lengths, jnp.concatenate([low, high]).astype(jnp.int32))
    count = len(spans)
    return (docs[:count] != docs[count:]).astype(jnp.float32)


def back_flags(doc_lengths, spans, tile):
    low = jnp.stack([lo * tile for lo, hi in spans])
    high = jnp.stack([hi * tile + tile for lo, hi in spans])
    docs = doc_index(doc_lengths, jnp.concatenate([low, high]).astype(jnp.int32))
    count = len(spans)
    return (docs[:count] != docs[count:]).astype(jnp.float32)


def wide(form, left, right):
    return jnp.einsum(form, left, right, precision=lax.Precision.HIGHEST)


def narrow(form, left, right):
    return jnp.einsum(form, left, right, preferred_element_type=jnp.float32)


def doc_index(doc_lengths, positions):
    starts = jnp.cumsum(doc_lengths) - doc_lengths
    return jnp.sum((starts[None, :] <= positions[:, None]).astype(jnp.int32), axis=1) - 1


def one_doc(doc_lengths, position):
    return doc_index(doc_lengths, jnp.reshape(position, (1,)))[0]


def masked_scores(query_block, key_block, mask, scale):
    raw = narrow("thd,uhd->htu", query_block, key_block) * scale
    return jnp.where(mask[None], raw, neg_large)


def key_terms(dscores, weights, query_block, grad_block, scale):
    key_part = narrow("htu,thd->uhd", dscores, query_block) * scale
    value_part = narrow("htu,thd->uhd", weights, grad_block)
    return (key_part, value_part)


def per_device(queries, keys, values, gain, doc_lengths, cotangent):
    tile, heads, width = queries.shape
    features = heads * lax.axis_size("head") * width
    scale = width ** (-0.5)
    base = lax.axis_index("ctx") * tile
    offsets = jnp.arange(tile, dtype=jnp.int32)
    own_pos = base + offsets
    own_doc = doc_index(doc_lengths, own_pos)
    prev_doc = one_doc(doc_lengths, base - 1)
    next_doc = one_doc(doc_lengths, base + tile)
    pair = jnp.stack([keys, values])
    arrived = [from_behind(pair, "ctx", shift) for shift in range(SPAN, 0, -1)]
    key_tiles = [piece[0] for piece in arrived] + [keys]
    value_tiles = [piece[1] for piece in arrived] + [values]
    masks = []
    for position in range(SPAN + 1):
        key_pos = base - (SPAN - position) * tile + offsets
        key_doc = doc_index(doc_lengths, key_pos)
        masks.append(
            (own_doc[:, None] == key_doc[None, :]) & (key_pos[None, :] <= own_pos[:, None])
        )
    score_list = [
        masked_scores(queries, key_tiles[position], masks[position], scale)
        for position in range(SPAN + 1)
    ]
    top = score_list[0].max(axis=-1)
    for position in range(1, SPAN + 1):
        top = jnp.maximum(top, score_list[position].max(axis=-1))
    total = jnp.zeros((heads, tile), jnp.float32)
    for position in range(SPAN + 1):
        total = total + jnp.sum(jnp.exp(score_list[position] - top[..., None]), axis=-1)
    log_total = top + jnp.log(total)
    prob_list = []
    weight_list = []
    soft_out = jnp.zeros((tile, heads, width), jnp.float32)
    for position in range(SPAN + 1):
        probs = jnp.exp(score_list[position] - log_total[..., None])
        weights = probs.astype(jnp.bfloat16)
        prob_list.append(probs)
        weight_list.append(weights)
        soft_out = soft_out + narrow("htu,uhd->thd", weights, value_tiles[position])
    same_tile = masks[SPAN].astype(jnp.float32)
    carried_prev = (own_doc == prev_doc).astype(jnp.float32)
    carried_next = (own_doc == next_doc).astype(jnp.float32)
    keep_first = (own_doc == own_doc[0])[:, None, None]
    query_wide = queries.astype(jnp.float32)
    attend = (narrow("thd,uhd->htu", queries, keys) * same_tile).astype(jnp.bfloat16)
    grad_wide = cotangent.astype(jnp.float32)
    row_dot = jnp.sum(grad_wide * soft_out, axis=-1).T
    query_soft = jnp.zeros((tile, heads, width), jnp.float32)
    dscore_list = []
    for position in range(SPAN + 1):
        dprobs = narrow("thd,uhd->htu", cotangent, value_tiles[position])
        dscores = (prob_list[position] * (dprobs - row_dot[..., None])).astype(jnp.bfloat16)
        query_soft = query_soft + narrow("htu,uhd->thd", dscores, key_tiles[position]) * scale
        dscore_list.append(dscores)
    parts = [
        key_terms(dscore_list[position], weight_list[position], queries, cotangent, scale)
        for position in range(SPAN + 1)
    ]
    outgoing = [
        jnp.stack(list(parts[SPAN - shift])).astype(jnp.bfloat16) for shift in range(1, SPAN + 1)
    ]
    place = lax.axis_index("ctx")
    need = min(-(-MAXDOC // tile), lax.axis_size("ctx"))
    near_states = [
        tile_state(key_tiles[position], value_tiles[position], doc_lengths,
                   base - (SPAN - position) * tile)
        for position in range(SPAN)
    ]
    near_spans = [(place - SPAN + position, place - SPAN + position) for position in range(SPAN)]
    incoming = fold_states(near_states, front_flags(doc_lengths, near_spans, tile))
    covered = SPAN
    returned = None
    while covered < need:
        (flag,) = front_flags(doc_lengths, [(place - covered, place - 1)], tile)
        if 2 * covered >= need:
            incoming, outgoing = lax.optimization_barrier((incoming, outgoing))
            returned = [
                from_behind(outgoing[shift - 1], "ctx", -shift) for shift in range(1, SPAN + 1)
            ]
        incoming = incoming + (1.0 - flag) * send_state(incoming, "ctx", covered)
        covered *= 2
    linear_out = (
        narrow("htu,uhd->thd", attend, values)
        + wide("thd,hde->the", query_wide, incoming) * carried_prev[:, None, None]
    )
    squares = lax.psum(jnp.sum(linear_out * linear_out, axis=(1, 2)), "head")
    inverse = lax.rsqrt(squares / features + norm_eps)
    mixed = (linear_out * inverse[:, None, None] * gain[None] + soft_out).astype(jnp.bfloat16)
    weighted = grad_wide * gain[None]
    projection = lax.psum(jnp.sum(weighted * linear_out, axis=(1, 2)), "head")
    inner = (
        inverse[:, None, None] * weighted
        - linear_out * (inverse**3 * projection / features)[:, None, None]
    ).astype(jnp.bfloat16)
    inner_wide = inner.astype(jnp.float32)
    back = (narrow("thd,uhd->htu", inner, values) * same_tile).astype(jnp.bfloat16)
    query_linear = (
        narrow("htu,uhd->thd", back, keys)
        + wide("the,hde->thd", inner_wide, incoming) * carried_prev[:, None, None]
    )
    tile_sum = narrow(
        "thd,the->hde", jnp.where(keep_first, queries, jnp.zeros_like(queries)), inner
    )
    key_soft, value_soft = parts[SPAN]
    if returned is None:
        returned = [
            from_behind(outgoing[shift - 1], "ctx", -shift) for shift in range(1, SPAN + 1)
        ]
    tile_sum, returned = lax.optimization_barrier((tile_sum, returned))
    for moved in returned:
        key_soft = key_soft + moved[0].astype(jnp.float32)
        value_soft = value_soft + moved[1].astype(jnp.float32)
    part = tile_sum
    covered = 1
    while 2 * covered < need:
        (flag,) = back_flags(doc_lengths, [(place, place + covered - 1)], tile)
        part = part + (1.0 - flag) * send_state(part, "ctx", -covered)
        covered *= 2
    later = send_state(part, "ctx", -1)
    if covered < need:
        (flag,) = back_flags(doc_lengths, [(place + 1, place + covered)], tile)
        later = later + (1.0 - flag) * send_state(part, "ctx", -1 - covered)
    key_linear = (
        narrow("htu,thd->uhd", back, queries)
        + wide("uhe,hde->uhd", values.astype(jnp.float32), later) * carried_next[:, None, None]
    )
    value_linear = (
        narrow("htu,the->uhe", attend, inner)
        + wide("uhd,hde->uhe", keys.astype(jnp.float32), later) * carried_next[:, None, None]
    )
    query_grad = (query_linear + query_soft).astype(jnp.bfloat16)
    key_grad = (key_linear + key_soft).astype(jnp.bfloat16)
    value_grad = (value_linear + value_soft).astype(jnp.bfloat16)
    return (mixed, query_grad, key_grad, value_grad)


def solution(mesh):
    placed = (
        P("ctx", "head", None),
        P("ctx", "head", None),
        P("ctx", "head", None),
        P("head", None),
        P(),
        P("ctx", "head", None),
    )
    return jax.shard_map(
        per_device,
        mesh=mesh,
        in_specs=placed,
        out_specs=(
            P("ctx", "head", None),
            P("ctx", "head", None),
            P("ctx", "head", None),
            P("ctx", "head", None),
        ),
        check_vma=False,
    )
```

```python
import jax
import jax.numpy as jnp
from jax import lax
from jax.sharding import PartitionSpec as P

SPAN = 2
MAXDOC = 2048


neg_large = -1e30
norm_eps = 1e-06


def from_behind(x, axis, by):
    devices = lax.axis_size(axis)
    pairs = [(i, i + by) for i in range(devices) if 0 <= i + by < devices]
    return lax.ppermute(x, axis, pairs)


def send_state(x, axis, by, exact=False):
    if exact:
        return from_behind(x, axis, by)
    return from_behind(x.astype(jnp.bfloat16), axis, by).astype(jnp.float32)


def tile_state(keys_t, values_t, doc_lengths, start):
    tile = keys_t.shape[0]
    docs = doc_index(doc_lengths, start + jnp.arange(tile, dtype=jnp.int32))
    keep = (docs == docs[tile - 1])[:, None, None]
    return narrow("uhd,uhe->hde", jnp.where(keep, keys_t, jnp.zeros_like(keys_t)), values_t)


def fold_states(pieces, flags):
    total = pieces[0]
    for piece, flag in zip(pieces[1:], flags[1:]):
        total = piece + (1.0 - flag) * total
    return total


def front_flags(doc_lengths, spans, tile):
    low = jnp.stack([lo * tile - 1 for lo, hi in spans])
    high = jnp.stack([hi * tile + tile - 1 for lo, hi in spans])
    docs = doc_index(doc_lengths, jnp.concatenate([low, high]).astype(jnp.int32))
    count = len(spans)
    return (docs[:count] != docs[count:]).astype(jnp.float32)


def back_flags(doc_lengths, spans, tile):
    low = jnp.stack([lo * tile for lo, hi in spans])
    high = jnp.stack([hi * tile + tile for lo, hi in spans])
    docs = doc_index(doc_lengths, jnp.concatenate([low, high]).astype(jnp.int32))
    count = len(spans)
    return (docs[:count] != docs[count:]).astype(jnp.float32)


def wide(form, left, right):
    return jnp.einsum(form, left, right, precision=lax.Precision.HIGHEST)


def narrow(form, left, right):
    return jnp.einsum(form, left, right, preferred_element_type=jnp.float32)


def doc_index(doc_lengths, positions):
    starts = jnp.cumsum(doc_lengths) - doc_lengths
    return jnp.sum((starts[None, :] <= positions[:, None]).astype(jnp.int32), axis=1) - 1


def one_doc(doc_lengths, position):
    return doc_index(doc_lengths, jnp.reshape(position, (1,)))[0]


def masked_scores(query_block, key_block, mask, scale):
    raw = narrow("thd,uhd->htu", query_block, key_block) * scale
    return jnp.where(mask[None], raw, neg_large)


def key_terms(dscores, weights, query_block, grad_block, scale):
    key_part = narrow("htu,thd->uhd", dscores, query_block) * scale
    value_part = narrow("htu,thd->uhd", weights, grad_block)
    return (key_part, value_part)


def per_device(queries, keys, values, gain, doc_lengths, cotangent):
    tile, heads, width = queries.shape
    features = heads * lax.axis_size("head") * width
    scale = width ** (-0.5)
    base = lax.axis_index("ctx") * tile
    offsets = jnp.arange(tile, dtype=jnp.int32)
    own_pos = base + offsets
    own_doc = doc_index(doc_lengths, own_pos)
    prev_doc = one_doc(doc_lengths, base - 1)
    next_doc = one_doc(doc_lengths, base + tile)
    pair = jnp.stack([keys, values])
    arrived = [from_behind(pair, "ctx", shift) for shift in range(SPAN, 0, -1)]
    key_tiles = [piece[0] for piece in arrived] + [keys]
    value_tiles = [piece[1] for piece in arrived] + [values]
    masks = []
    for position in range(SPAN + 1):
        key_pos = base - (SPAN - position) * tile + offsets
        key_doc = doc_index(doc_lengths, key_pos)
        masks.append(
            (own_doc[:, None] == key_doc[None, :]) & (key_pos[None, :] <= own_pos[:, None])
        )
    score_list = [
        masked_scores(queries, key_tiles[position], masks[position], scale)
        for position in range(SPAN + 1)
    ]
    top = score_list[0].max(axis=-1)
    for position in range(1, SPAN + 1):
        top = jnp.maximum(top, score_list[position].max(axis=-1))
    total = jnp.zeros((heads, tile), jnp.float32)
    for position in range(SPAN + 1):
        total = total + jnp.sum(jnp.exp(score_list[position] - top[..., None]), axis=-1)
    log_total = top + jnp.log(total)
    prob_list = []
    weight_list = []
    soft_out = jnp.zeros((tile, heads, width), jnp.float32)
    for position in range(SPAN + 1):
        probs = jnp.exp(score_list[position] - log_total[..., None])
        weights = probs.astype(jnp.bfloat16)
        prob_list.append(probs)
        weight_list.append(weights)
        soft_out = soft_out + narrow("htu,uhd->thd", weights, value_tiles[position])
    same_tile = masks[SPAN].astype(jnp.float32)
    carried_prev = (own_doc == prev_doc).astype(jnp.float32)
    carried_next = (own_doc == next_doc).astype(jnp.float32)
    keep_first = (own_doc == own_doc[0])[:, None, None]
    query_wide = queries.astype(jnp.float32)
    attend = (narrow("thd,uhd->htu", queries, keys) * same_tile).astype(jnp.bfloat16)
    grad_wide = cotangent.astype(jnp.float32)
    row_dot = jnp.sum(grad_wide * soft_out, axis=-1).T
    query_soft = jnp.zeros((tile, heads, width), jnp.float32)
    dscore_list = []
    for position in range(SPAN + 1):
        dprobs = narrow("thd,uhd->htu", cotangent, value_tiles[position])
        dscores = (prob_list[position] * (dprobs - row_dot[..., None])).astype(jnp.bfloat16)
        query_soft = query_soft + narrow("htu,uhd->thd", dscores, key_tiles[position]) * scale
        dscore_list.append(dscores)
    parts = [
        key_terms(dscore_list[position], weight_list[position], queries, cotangent, scale)
        for position in range(SPAN + 1)
    ]
    outgoing = [
        jnp.stack(list(parts[SPAN - shift])).astype(jnp.bfloat16) for shift in range(1, SPAN + 1)
    ]
    place = lax.axis_index("ctx")
    need = min(-(-MAXDOC // tile), lax.axis_size("ctx"))
    near_states = [
        tile_state(key_tiles[position], value_tiles[position], doc_lengths,
                   base - (SPAN - position) * tile)
        for position in range(SPAN)
    ]
    near_spans = [(place - SPAN + position, place - SPAN + position) for position in range(SPAN)]
    incoming = fold_states(near_states, front_flags(doc_lengths, near_spans, tile))
    covered = SPAN
    returned = None
    while covered < need:
        (flag,) = front_flags(doc_lengths, [(place - covered, place - 1)], tile)
        if 2 * covered >= need:
            incoming, outgoing = lax.optimization_barrier((incoming, outgoing))
            returned = [
                from_behind(outgoing[shift - 1], "ctx", -shift) for shift in range(1, SPAN + 1)
            ]
        incoming = incoming + (1.0 - flag) * send_state(
            incoming, "ctx", covered, exact=2 * covered >= need
        )
        covered *= 2
    linear_out = (
        narrow("htu,uhd->thd", attend, values)
        + wide("thd,hde->the", query_wide, incoming) * carried_prev[:, None, None]
    )
    squares = lax.psum(jnp.sum(linear_out * linear_out, axis=(1, 2)), "head")
    inverse = lax.rsqrt(squares / features + norm_eps)
    mixed = (linear_out * inverse[:, None, None] * gain[None] + soft_out).astype(jnp.bfloat16)
    weighted = grad_wide * gain[None]
    projection = lax.psum(jnp.sum(weighted * linear_out, axis=(1, 2)), "head")
    inner = (
        inverse[:, None, None] * weighted
        - linear_out * (inverse**3 * projection / features)[:, None, None]
    ).astype(jnp.bfloat16)
    inner_wide = inner.astype(jnp.float32)
    back = (narrow("thd,uhd->htu", inner, values) * same_tile).astype(jnp.bfloat16)
    query_linear = (
        narrow("htu,uhd->thd", back, keys)
        + wide("the,hde->thd", inner_wide, incoming) * carried_prev[:, None, None]
    )
    tile_sum = narrow(
        "thd,the->hde", jnp.where(keep_first, queries, jnp.zeros_like(queries)), inner
    )
    key_soft, value_soft = parts[SPAN]
    if returned is None:
        returned = [
            from_behind(outgoing[shift - 1], "ctx", -shift) for shift in range(1, SPAN + 1)
        ]
    tile_sum, returned = lax.optimization_barrier((tile_sum, returned))
    for moved in returned:
        key_soft = key_soft + moved[0].astype(jnp.float32)
        value_soft = value_soft + moved[1].astype(jnp.float32)
    part = tile_sum
    covered = 1
    while 2 * covered < need:
        (flag,) = back_flags(doc_lengths, [(place, place + covered - 1)], tile)
        part = part + (1.0 - flag) * send_state(part, "ctx", -covered)
        covered *= 2
    later = send_state(part, "ctx", -1, exact=True)
    if covered < need:
        (flag,) = back_flags(doc_lengths, [(place + 1, place + covered)], tile)
        later = later + (1.0 - flag) * send_state(part, "ctx", -1 - covered, exact=True)
    key_linear = (
        narrow("htu,thd->uhd", back, queries)
        + wide("uhe,hde->uhd", values.astype(jnp.float32), later) * carried_next[:, None, None]
    )
    value_linear = (
        narrow("htu,the->uhe", attend, inner)
        + wide("uhd,hde->uhe", keys.astype(jnp.float32), later) * carried_next[:, None, None]
    )
    query_grad = (query_linear + query_soft).astype(jnp.bfloat16)
    key_grad = (key_linear + key_soft).astype(jnp.bfloat16)
    value_grad = (value_linear + value_soft).astype(jnp.bfloat16)
    return (mixed, query_grad, key_grad, value_grad)


def solution(mesh):
    placed = (
        P("ctx", "head", None),
        P("ctx", "head", None),
        P("ctx", "head", None),
        P("head", None),
        P(),
        P("ctx", "head", None),
    )
    return jax.shard_map(
        per_device,
        mesh=mesh,
        in_specs=placed,
        out_specs=(
            P("ctx", "head", None),
            P("ctx", "head", None),
            P("ctx", "head", None),
            P("ctx", "head", None),
        ),
        check_vma=False,
    )
```

```python
import jax
import jax.numpy as jnp
from jax import lax
from jax.sharding import PartitionSpec as P

SPAN = 2
MAXDOC = 2048


neg_large = -1e30
norm_eps = 1e-06


def from_behind(x, axis, by):
    devices = lax.axis_size(axis)
    pairs = [(i, i + by) for i in range(devices) if 0 <= i + by < devices]
    return lax.ppermute(x, axis, pairs)


def send_state(x, axis, by):
    return from_behind(x.astype(jnp.bfloat16), axis, by).astype(jnp.float32)


def tile_state(keys_t, values_t, doc_lengths, start):
    tile = keys_t.shape[0]
    docs = doc_index(doc_lengths, start + jnp.arange(tile, dtype=jnp.int32))
    keep = (docs == docs[tile - 1])[:, None, None]
    return narrow("uhd,uhe->hde", jnp.where(keep, keys_t, jnp.zeros_like(keys_t)), values_t)


def fold_states(pieces, flags):
    total = pieces[0]
    for piece, flag in zip(pieces[1:], flags[1:]):
        total = piece + (1.0 - flag) * total
    return total


def front_flags(doc_lengths, spans, tile):
    low = jnp.stack([lo * tile - 1 for lo, hi in spans])
    high = jnp.stack([hi * tile + tile - 1 for lo, hi in spans])
    docs = doc_index(doc_lengths, jnp.concatenate([low, high]).astype(jnp.int32))
    count = len(spans)
    return (docs[:count] != docs[count:]).astype(jnp.float32)


def back_flags(doc_lengths, spans, tile):
    low = jnp.stack([lo * tile for lo, hi in spans])
    high = jnp.stack([hi * tile + tile for lo, hi in spans])
    docs = doc_index(doc_lengths, jnp.concatenate([low, high]).astype(jnp.int32))
    count = len(spans)
    return (docs[:count] != docs[count:]).astype(jnp.float32)


def wide(form, left, right):
    return jnp.einsum(form, left, right, precision=lax.Precision.HIGHEST)


def narrow(form, left, right):
    return jnp.einsum(form, left, right, preferred_element_type=jnp.float32)


def doc_index(doc_lengths, positions):
    starts = jnp.cumsum(doc_lengths) - doc_lengths
    return jnp.sum((starts[None, :] <= positions[:, None]).astype(jnp.int32), axis=1) - 1


def one_doc(doc_lengths, position):
    return doc_index(doc_lengths, jnp.reshape(position, (1,)))[0]


def masked_scores(query_block, key_block, mask, scale):
    raw = narrow("thd,uhd->htu", query_block, key_block) * scale
    return jnp.where(mask[None], raw, neg_large)


def key_terms(dscores, weights, query_block, grad_block, scale):
    key_part = narrow("htu,thd->uhd", dscores, query_block) * scale
    value_part = narrow("htu,thd->uhd", weights, grad_block)
    return (key_part, value_part)


def per_device(queries, keys, values, gain, doc_lengths, cotangent):
    tile, heads, width = queries.shape
    features = heads * lax.axis_size("head") * width
    scale = width ** (-0.5)
    base = lax.axis_index("ctx") * tile
    offsets = jnp.arange(tile, dtype=jnp.int32)
    own_pos = base + offsets
    own_doc = doc_index(doc_lengths, own_pos)
    prev_doc = one_doc(doc_lengths, base - 1)
    next_doc = one_doc(doc_lengths, base + tile)
    pair = jnp.stack([keys, values])
    asks = jnp.stack([queries, cotangent])
    later_asks = [from_behind(asks, "ctx", -shift) for shift in range(1, SPAN + 1)]
    arrived = [from_behind(pair, "ctx", shift) for shift in range(SPAN, 0, -1)]
    key_tiles = [piece[0] for piece in arrived] + [keys]
    value_tiles = [piece[1] for piece in arrived] + [values]
    masks = []
    for position in range(SPAN + 1):
        key_pos = base - (SPAN - position) * tile + offsets
        key_doc = doc_index(doc_lengths, key_pos)
        masks.append(
            (own_doc[:, None] == key_doc[None, :]) & (key_pos[None, :] <= own_pos[:, None])
        )
    score_list = [
        masked_scores(queries, key_tiles[position], masks[position], scale)
        for position in range(SPAN + 1)
    ]
    top = score_list[0].max(axis=-1)
    for position in range(1, SPAN + 1):
        top = jnp.maximum(top, score_list[position].max(axis=-1))
    total = jnp.zeros((heads, tile), jnp.float32)
    for position in range(SPAN + 1):
        total = total + jnp.sum(jnp.exp(score_list[position] - top[..., None]), axis=-1)
    log_total = top + jnp.log(total)
    prob_list = []
    weight_list = []
    soft_out = jnp.zeros((tile, heads, width), jnp.float32)
    for position in range(SPAN + 1):
        probs = jnp.exp(score_list[position] - log_total[..., None])
        weights = probs.astype(jnp.bfloat16)
        prob_list.append(probs)
        weight_list.append(weights)
        soft_out = soft_out + narrow("htu,uhd->thd", weights, value_tiles[position])
    same_tile = masks[SPAN].astype(jnp.float32)
    carried_prev = (own_doc == prev_doc).astype(jnp.float32)
    carried_next = (own_doc == next_doc).astype(jnp.float32)
    keep_first = (own_doc == own_doc[0])[:, None, None]
    query_wide = queries.astype(jnp.float32)
    attend = (narrow("thd,uhd->htu", queries, keys) * same_tile).astype(jnp.bfloat16)
    grad_wide = cotangent.astype(jnp.float32)
    row_dot = jnp.sum(grad_wide * soft_out, axis=-1).T
    query_soft = jnp.zeros((tile, heads, width), jnp.float32)
    dscore_list = []
    for position in range(SPAN + 1):
        dprobs = narrow("thd,uhd->htu", cotangent, value_tiles[position])
        dscores = (prob_list[position] * (dprobs - row_dot[..., None])).astype(jnp.bfloat16)
        query_soft = query_soft + narrow("htu,uhd->thd", dscores, key_tiles[position]) * scale
        dscore_list.append(dscores)
    key_soft, value_soft = key_terms(
        dscore_list[SPAN], weight_list[SPAN], queries, cotangent, scale
    )
    stats = jnp.stack([log_total, row_dot])
    later_stats = [from_behind(stats, "ctx", -shift) for shift in range(1, SPAN + 1)]
    place = lax.axis_index("ctx")
    need = min(-(-MAXDOC // tile), lax.axis_size("ctx"))
    near_states = [
        tile_state(key_tiles[position], value_tiles[position], doc_lengths,
                   base - (SPAN - position) * tile)
        for position in range(SPAN)
    ]
    near_spans = [(place - SPAN + position, place - SPAN + position) for position in range(SPAN)]
    incoming = fold_states(near_states, front_flags(doc_lengths, near_spans, tile))
    covered = SPAN
    while covered < need:
        (flag,) = front_flags(doc_lengths, [(place - covered, place - 1)], tile)
        incoming = incoming + (1.0 - flag) * send_state(incoming, "ctx", covered)
        covered *= 2
    linear_out = (
        narrow("htu,uhd->thd", attend, values)
        + wide("thd,hde->the", query_wide, incoming) * carried_prev[:, None, None]
    )
    squares = lax.psum(jnp.sum(linear_out * linear_out, axis=(1, 2)), "head")
    inverse = lax.rsqrt(squares / features + norm_eps)
    mixed = (linear_out * inverse[:, None, None] * gain[None] + soft_out).astype(jnp.bfloat16)
    weighted = grad_wide * gain[None]
    projection = lax.psum(jnp.sum(weighted * linear_out, axis=(1, 2)), "head")
    inner = (
        inverse[:, None, None] * weighted
        - linear_out * (inverse**3 * projection / features)[:, None, None]
    ).astype(jnp.bfloat16)
    inner_wide = inner.astype(jnp.float32)
    back = (narrow("thd,uhd->htu", inner, values) * same_tile).astype(jnp.bfloat16)
    query_linear = (
        narrow("htu,uhd->thd", back, keys)
        + wide("the,hde->thd", inner_wide, incoming) * carried_prev[:, None, None]
    )
    tile_sum = narrow(
        "thd,the->hde", jnp.where(keep_first, queries, jnp.zeros_like(queries)), inner
    )
    tile_sum, later_asks, later_stats = lax.optimization_barrier(
        (tile_sum, later_asks, later_stats)
    )
    total_len = lax.axis_size("ctx") * tile
    for shift in range(1, SPAN + 1):
        query_t = later_asks[shift - 1][0]
        grad_t = later_asks[shift - 1][1]
        lse_t = later_stats[shift - 1][0]
        dot_t = later_stats[shift - 1][1]
        query_pos = own_pos + shift * tile
        query_doc = doc_index(doc_lengths, query_pos)
        mask = (
            (query_doc[:, None] == own_doc[None, :])
            & (own_pos[None, :] <= query_pos[:, None])
            & (query_pos[:, None] < total_len)
        )
        probs = jnp.exp(masked_scores(query_t, keys, mask, scale) - lse_t[..., None])
        weights = probs.astype(jnp.bfloat16)
        dprobs = narrow("thd,uhd->htu", grad_t, values)
        dscores = (probs * (dprobs - dot_t[..., None])).astype(jnp.bfloat16)
        key_part, value_part = key_terms(dscores, weights, query_t, grad_t, scale)
        key_soft = key_soft + key_part
        value_soft = value_soft + value_part
    part = tile_sum
    covered = 1
    while 2 * covered < need:
        (flag,) = back_flags(doc_lengths, [(place, place + covered - 1)], tile)
        part = part + (1.0 - flag) * send_state(part, "ctx", -covered)
        covered *= 2
    later = send_state(part, "ctx", -1)
    if covered < need:
        (flag,) = back_flags(doc_lengths, [(place + 1, place + covered)], tile)
        later = later + (1.0 - flag) * send_state(part, "ctx", -1 - covered)
    key_linear = (
        narrow("htu,thd->uhd", back, queries)
        + wide("uhe,hde->uhd", values.astype(jnp.float32), later) * carried_next[:, None, None]
    )
    value_linear = (
        narrow("htu,the->uhe", attend, inner)
        + wide("uhd,hde->uhe", keys.astype(jnp.float32), later) * carried_next[:, None, None]
    )
    query_grad = (query_linear + query_soft).astype(jnp.bfloat16)
    key_grad = (key_linear + key_soft).astype(jnp.bfloat16)
    value_grad = (value_linear + value_soft).astype(jnp.bfloat16)
    return (mixed, query_grad, key_grad, value_grad)


def solution(mesh):
    placed = (
        P("ctx", "head", None),
        P("ctx", "head", None),
        P("ctx", "head", None),
        P("head", None),
        P(),
        P("ctx", "head", None),
    )
    return jax.shard_map(
        per_device,
        mesh=mesh,
        in_specs=placed,
        out_specs=(
            P("ctx", "head", None),
            P("ctx", "head", None),
            P("ctx", "head", None),
            P("ctx", "head", None),
        ),
        check_vma=False,
    )
```

```python
import jax
import jax.numpy as jnp
from jax import lax
from jax.sharding import PartitionSpec as P

SPAN = 2
MAXDOC = 2048


neg_large = -1e30
norm_eps = 1e-06


def from_behind(x, axis, by):
    devices = lax.axis_size(axis)
    pairs = [(i, i + by) for i in range(devices) if 0 <= i + by < devices]
    return lax.ppermute(x, axis, pairs)


def send_state(x, axis, by):
    return from_behind(x.astype(jnp.bfloat16), axis, by).astype(jnp.float32)


def tile_state(keys_t, values_t, doc_lengths, start):
    tile = keys_t.shape[0]
    docs = doc_index(doc_lengths, start + jnp.arange(tile, dtype=jnp.int32))
    keep = (docs == docs[tile - 1])[:, None, None]
    return narrow("uhd,uhe->hde", jnp.where(keep, keys_t, jnp.zeros_like(keys_t)), values_t)


def fold_states(pieces, flags):
    total = pieces[0]
    for piece, flag in zip(pieces[1:], flags[1:]):
        total = piece + (1.0 - flag) * total
    return total


def front_flags(doc_lengths, spans, tile):
    low = jnp.stack([lo * tile - 1 for lo, hi in spans])
    high = jnp.stack([hi * tile + tile - 1 for lo, hi in spans])
    docs = doc_index(doc_lengths, jnp.concatenate([low, high]).astype(jnp.int32))
    count = len(spans)
    return (docs[:count] != docs[count:]).astype(jnp.float32)


def back_flags(doc_lengths, spans, tile):
    low = jnp.stack([lo * tile for lo, hi in spans])
    high = jnp.stack([hi * tile + tile for lo, hi in spans])
    docs = doc_index(doc_lengths, jnp.concatenate([low, high]).astype(jnp.int32))
    count = len(spans)
    return (docs[:count] != docs[count:]).astype(jnp.float32)


def wide(form, left, right):
    return jnp.einsum(form, left, right, precision=lax.Precision.HIGHEST)


def narrow(form, left, right):
    return jnp.einsum(form, left, right, preferred_element_type=jnp.float32)


def doc_index(doc_lengths, positions):
    starts = jnp.cumsum(doc_lengths) - doc_lengths
    return jnp.sum((starts[None, :] <= positions[:, None]).astype(jnp.int32), axis=1) - 1


def one_doc(doc_lengths, position):
    return doc_index(doc_lengths, jnp.reshape(position, (1,)))[0]


def masked_scores(query_block, key_block, mask, scale):
    raw = narrow("thd,uhd->htu", query_block, key_block) * scale
    return jnp.where(mask[None], raw, neg_large)


def key_terms(dscores, weights, query_block, grad_block, scale):
    key_part = narrow("htu,thd->uhd", dscores, query_block) * scale
    value_part = narrow("htu,thd->uhd", weights, grad_block)
    return (key_part, value_part)


def per_device(queries, keys, values, gain, doc_lengths, cotangent):
    tile, heads, width = queries.shape
    features = heads * lax.axis_size("head") * width
    scale = width ** (-0.5)
    base = lax.axis_index("ctx") * tile
    offsets = jnp.arange(tile, dtype=jnp.int32)
    own_pos = base + offsets
    own_doc = doc_index(doc_lengths, own_pos)
    prev_doc = one_doc(doc_lengths, base - 1)
    next_doc = one_doc(doc_lengths, base + tile)
    pair = jnp.stack([keys, values])
    arrived = [from_behind(pair, "ctx", shift) for shift in range(SPAN, 0, -1)]
    key_tiles = [piece[0] for piece in arrived] + [keys]
    value_tiles = [piece[1] for piece in arrived] + [values]
    masks = []
    for position in range(SPAN + 1):
        key_pos = base - (SPAN - position) * tile + offsets
        key_doc = doc_index(doc_lengths, key_pos)
        masks.append(
            (own_doc[:, None] == key_doc[None, :]) & (key_pos[None, :] <= own_pos[:, None])
        )
    score_list = [
        masked_scores(queries, key_tiles[position], masks[position], scale)
        for position in range(SPAN + 1)
    ]
    top = score_list[0].max(axis=-1)
    for position in range(1, SPAN + 1):
        top = jnp.maximum(top, score_list[position].max(axis=-1))
    total = jnp.zeros((heads, tile), jnp.float32)
    for position in range(SPAN + 1):
        total = total + jnp.sum(jnp.exp(score_list[position] - top[..., None]), axis=-1)
    log_total = top + jnp.log(total)
    prob_list = []
    weight_list = []
    soft_out = jnp.zeros((tile, heads, width), jnp.float32)
    for position in range(SPAN + 1):
        probs = jnp.exp(score_list[position] - log_total[..., None])
        weights = probs.astype(jnp.bfloat16)
        prob_list.append(probs)
        weight_list.append(weights)
        soft_out = soft_out + narrow("htu,uhd->thd", weights, value_tiles[position])
    same_tile = masks[SPAN].astype(jnp.float32)
    carried_prev = (own_doc == prev_doc).astype(jnp.float32)
    carried_next = (own_doc == next_doc).astype(jnp.float32)
    keep_first = (own_doc == own_doc[0])[:, None, None]
    query_wide = queries.astype(jnp.float32)
    attend = (narrow("thd,uhd->htu", queries, keys) * same_tile).astype(jnp.bfloat16)
    grad_wide = cotangent.astype(jnp.float32)
    row_dot = jnp.sum(grad_wide * soft_out, axis=-1).T
    query_soft = jnp.zeros((tile, heads, width), jnp.float32)
    dscore_list = []
    for position in range(SPAN + 1):
        dprobs = narrow("thd,uhd->htu", cotangent, value_tiles[position])
        dscores = (prob_list[position] * (dprobs - row_dot[..., None])).astype(jnp.bfloat16)
        query_soft = query_soft + narrow("htu,uhd->thd", dscores, key_tiles[position]) * scale
        dscore_list.append(dscores)
    parts = [
        key_terms(dscore_list[position], weight_list[position], queries, cotangent, scale)
        for position in range(SPAN + 1)
    ]
    outgoing = [
        jnp.stack(list(parts[SPAN - shift])).astype(jnp.bfloat16) for shift in range(1, SPAN + 1)
    ]
    place = lax.axis_index("ctx")
    need = min(-(-MAXDOC // tile), lax.axis_size("ctx"))
    near_states = [
        tile_state(key_tiles[position], value_tiles[position], doc_lengths,
                   base - (SPAN - position) * tile)
        for position in range(SPAN)
    ]
    near_spans = [(place - SPAN + position, place - SPAN + position) for position in range(SPAN)]
    incoming = fold_states(near_states, front_flags(doc_lengths, near_spans, tile))
    covered = SPAN
    returned = None
    while covered < need:
        (flag,) = front_flags(doc_lengths, [(place - covered, place - 1)], tile)
        if 2 * covered >= need:
            incoming, outgoing = lax.optimization_barrier((incoming, outgoing))
            returned = [
                from_behind(outgoing[shift - 1], "ctx", -shift) for shift in range(1, SPAN + 1)
            ]
        incoming = incoming + (1.0 - flag) * send_state(incoming, "ctx", covered)
        covered *= 2
    linear_out = (
        narrow("htu,uhd->thd", attend, values)
        + wide("thd,hde->the", query_wide, incoming) * carried_prev[:, None, None]
    )
    squares = lax.psum(jnp.sum(linear_out * linear_out, axis=(1, 2)), "head")
    inverse = lax.rsqrt(squares / features + norm_eps)
    mixed = (linear_out * inverse[:, None, None] * gain[None] + soft_out).astype(jnp.bfloat16)
    weighted = grad_wide * gain[None]
    projection = lax.psum(jnp.sum(weighted * linear_out, axis=(1, 2)), "head")
    inner = (
        inverse[:, None, None] * weighted
        - linear_out * (inverse**3 * projection / features)[:, None, None]
    ).astype(jnp.bfloat16)
    inner_wide = inner.astype(jnp.float32)
    back = (narrow("thd,uhd->htu", inner, values) * same_tile).astype(jnp.bfloat16)
    query_linear = (
        narrow("htu,uhd->thd", back, keys)
        + wide("the,hde->thd", inner_wide, incoming) * carried_prev[:, None, None]
    )
    tile_sum = narrow(
        "thd,the->hde", jnp.where(keep_first, queries, jnp.zeros_like(queries)), inner
    )
    key_soft, value_soft = parts[SPAN]
    if returned is None:
        returned = [
            from_behind(outgoing[shift - 1], "ctx", -shift) for shift in range(1, SPAN + 1)
        ]
    part = tile_sum
    covered = 1
    while 2 * covered < need:
        (flag,) = back_flags(doc_lengths, [(place, place + covered - 1)], tile)
        received = send_state(part, "ctx", -covered)
        if covered == 1:
            received, returned = lax.optimization_barrier((received, returned))
        part = part + (1.0 - flag) * received
        covered *= 2
    for moved in returned:
        key_soft = key_soft + moved[0].astype(jnp.float32)
        value_soft = value_soft + moved[1].astype(jnp.float32)
    later = send_state(part, "ctx", -1)
    if covered < need:
        (flag,) = back_flags(doc_lengths, [(place + 1, place + covered)], tile)
        later = later + (1.0 - flag) * send_state(part, "ctx", -1 - covered)
    key_linear = (
        narrow("htu,thd->uhd", back, queries)
        + wide("uhe,hde->uhd", values.astype(jnp.float32), later) * carried_next[:, None, None]
    )
    value_linear = (
        narrow("htu,the->uhe", attend, inner)
        + wide("uhd,hde->uhe", keys.astype(jnp.float32), later) * carried_next[:, None, None]
    )
    query_grad = (query_linear + query_soft).astype(jnp.bfloat16)
    key_grad = (key_linear + key_soft).astype(jnp.bfloat16)
    value_grad = (value_linear + value_soft).astype(jnp.bfloat16)
    return (mixed, query_grad, key_grad, value_grad)


def solution(mesh):
    placed = (
        P("ctx", "head", None),
        P("ctx", "head", None),
        P("ctx", "head", None),
        P("head", None),
        P(),
        P("ctx", "head", None),
    )
    return jax.shard_map(
        per_device,
        mesh=mesh,
        in_specs=placed,
        out_specs=(
            P("ctx", "head", None),
            P("ctx", "head", None),
            P("ctx", "head", None),
            P("ctx", "head", None),
        ),
        check_vma=False,
    )
```

```python
import jax
import jax.numpy as jnp
from jax import lax
from jax.sharding import PartitionSpec as P

SPAN = 2
MAXDOC = 2048


neg_large = -1e30
norm_eps = 1e-06


def from_behind(x, axis, by):
    devices = lax.axis_size(axis)
    pairs = [(i, i + by) for i in range(devices) if 0 <= i + by < devices]
    return lax.ppermute(x, axis, pairs)


def relay(x, axis, by, sources):
    devices = lax.axis_size(axis)
    return lax.ppermute(x, axis, [(i, i + by) for i in sources if 0 <= i + by < devices])


def window_tiles(pair, axis):
    devices = lax.axis_size(axis)
    if SPAN != 2 or devices % 2:
        return [from_behind(pair, axis, shift) for shift in range(SPAN, 0, -1)]
    even = range(0, devices, 2)
    one_back = from_behind(pair, axis, 1)
    from_even = relay(pair, axis, 2, even)
    relayed = relay(one_back, axis, 1, even)
    two_back = jnp.where(lax.axis_index(axis) % 2 == 0, from_even, relayed)
    return [two_back, one_back]


def send_state(x, axis, by):
    return from_behind(x.astype(jnp.bfloat16), axis, by).astype(jnp.float32)


def tile_state(keys_t, values_t, doc_lengths, start):
    tile = keys_t.shape[0]
    docs = doc_index(doc_lengths, start + jnp.arange(tile, dtype=jnp.int32))
    keep = (docs == docs[tile - 1])[:, None, None]
    return narrow("uhd,uhe->hde", jnp.where(keep, keys_t, jnp.zeros_like(keys_t)), values_t)


def fold_states(pieces, flags):
    total = pieces[0]
    for piece, flag in zip(pieces[1:], flags[1:]):
        total = piece + (1.0 - flag) * total
    return total


def front_flags(doc_lengths, spans, tile):
    low = jnp.stack([lo * tile - 1 for lo, hi in spans])
    high = jnp.stack([hi * tile + tile - 1 for lo, hi in spans])
    docs = doc_index(doc_lengths, jnp.concatenate([low, high]).astype(jnp.int32))
    count = len(spans)
    return (docs[:count] != docs[count:]).astype(jnp.float32)


def back_flags(doc_lengths, spans, tile):
    low = jnp.stack([lo * tile for lo, hi in spans])
    high = jnp.stack([hi * tile + tile for lo, hi in spans])
    docs = doc_index(doc_lengths, jnp.concatenate([low, high]).astype(jnp.int32))
    count = len(spans)
    return (docs[:count] != docs[count:]).astype(jnp.float32)


def wide(form, left, right):
    return jnp.einsum(form, left, right, precision=lax.Precision.HIGHEST)


def narrow(form, left, right):
    return jnp.einsum(form, left, right, preferred_element_type=jnp.float32)


def doc_index(doc_lengths, positions):
    starts = jnp.cumsum(doc_lengths) - doc_lengths
    return jnp.sum((starts[None, :] <= positions[:, None]).astype(jnp.int32), axis=1) - 1


def one_doc(doc_lengths, position):
    return doc_index(doc_lengths, jnp.reshape(position, (1,)))[0]


def masked_scores(query_block, key_block, mask, scale):
    raw = narrow("thd,uhd->htu", query_block, key_block) * scale
    return jnp.where(mask[None], raw, neg_large)


def key_terms(dscores, weights, query_block, grad_block, scale):
    key_part = narrow("htu,thd->uhd", dscores, query_block) * scale
    value_part = narrow("htu,thd->uhd", weights, grad_block)
    return (key_part, value_part)


def per_device(queries, keys, values, gain, doc_lengths, cotangent):
    tile, heads, width = queries.shape
    features = heads * lax.axis_size("head") * width
    scale = width ** (-0.5)
    base = lax.axis_index("ctx") * tile
    offsets = jnp.arange(tile, dtype=jnp.int32)
    own_pos = base + offsets
    own_doc = doc_index(doc_lengths, own_pos)
    prev_doc = one_doc(doc_lengths, base - 1)
    next_doc = one_doc(doc_lengths, base + tile)
    pair = jnp.stack([keys, values])
    arrived = window_tiles(pair, "ctx")
    key_tiles = [piece[0] for piece in arrived] + [keys]
    value_tiles = [piece[1] for piece in arrived] + [values]
    masks = []
    for position in range(SPAN + 1):
        key_pos = base - (SPAN - position) * tile + offsets
        key_doc = doc_index(doc_lengths, key_pos)
        masks.append(
            (own_doc[:, None] == key_doc[None, :]) & (key_pos[None, :] <= own_pos[:, None])
        )
    score_list = [
        masked_scores(queries, key_tiles[position], masks[position], scale)
        for position in range(SPAN + 1)
    ]
    top = score_list[0].max(axis=-1)
    for position in range(1, SPAN + 1):
        top = jnp.maximum(top, score_list[position].max(axis=-1))
    total = jnp.zeros((heads, tile), jnp.float32)
    for position in range(SPAN + 1):
        total = total + jnp.sum(jnp.exp(score_list[position] - top[..., None]), axis=-1)
    log_total = top + jnp.log(total)
    prob_list = []
    weight_list = []
    soft_out = jnp.zeros((tile, heads, width), jnp.float32)
    for position in range(SPAN + 1):
        probs = jnp.exp(score_list[position] - log_total[..., None])
        weights = probs.astype(jnp.bfloat16)
        prob_list.append(probs)
        weight_list.append(weights)
        soft_out = soft_out + narrow("htu,uhd->thd", weights, value_tiles[position])
    same_tile = masks[SPAN].astype(jnp.float32)
    carried_prev = (own_doc == prev_doc).astype(jnp.float32)
    carried_next = (own_doc == next_doc).astype(jnp.float32)
    keep_first = (own_doc == own_doc[0])[:, None, None]
    query_wide = queries.astype(jnp.float32)
    attend = (narrow("thd,uhd->htu", queries, keys) * same_tile).astype(jnp.bfloat16)
    grad_wide = cotangent.astype(jnp.float32)
    row_dot = jnp.sum(grad_wide * soft_out, axis=-1).T
    query_soft = jnp.zeros((tile, heads, width), jnp.float32)
    dscore_list = []
    for position in range(SPAN + 1):
        dprobs = narrow("thd,uhd->htu", cotangent, value_tiles[position])
        dscores = (prob_list[position] * (dprobs - row_dot[..., None])).astype(jnp.bfloat16)
        query_soft = query_soft + narrow("htu,uhd->thd", dscores, key_tiles[position]) * scale
        dscore_list.append(dscores)
    parts = [
        key_terms(dscore_list[position], weight_list[position], queries, cotangent, scale)
        for position in range(SPAN + 1)
    ]
    outgoing = [
        jnp.stack(list(parts[SPAN - shift])).astype(jnp.bfloat16) for shift in range(1, SPAN + 1)
    ]
    place = lax.axis_index("ctx")
    need = min(-(-MAXDOC // tile), lax.axis_size("ctx"))
    near_states = [
        tile_state(key_tiles[position], value_tiles[position], doc_lengths,
                   base - (SPAN - position) * tile)
        for position in range(SPAN)
    ]
    near_spans = [(place - SPAN + position, place - SPAN + position) for position in range(SPAN)]
    incoming = fold_states(near_states, front_flags(doc_lengths, near_spans, tile))
    covered = SPAN
    returned = None
    while covered < need:
        (flag,) = front_flags(doc_lengths, [(place - covered, place - 1)], tile)
        if 2 * covered >= need:
            incoming, outgoing = lax.optimization_barrier((incoming, outgoing))
            returned = [
                from_behind(outgoing[shift - 1], "ctx", -shift) for shift in range(1, SPAN + 1)
            ]
        incoming = incoming + (1.0 - flag) * send_state(incoming, "ctx", covered)
        covered *= 2
    linear_out = (
        narrow("htu,uhd->thd", attend, values)
        + wide("thd,hde->the", query_wide, incoming) * carried_prev[:, None, None]
    )
    squares = lax.psum(jnp.sum(linear_out * linear_out, axis=(1, 2)), "head")
    inverse = lax.rsqrt(squares / features + norm_eps)
    mixed = (linear_out * inverse[:, None, None] * gain[None] + soft_out).astype(jnp.bfloat16)
    weighted = grad_wide * gain[None]
    projection = lax.psum(jnp.sum(weighted * linear_out, axis=(1, 2)), "head")
    inner = (
        inverse[:, None, None] * weighted
        - linear_out * (inverse**3 * projection / features)[:, None, None]
    ).astype(jnp.bfloat16)
    inner_wide = inner.astype(jnp.float32)
    back = (narrow("thd,uhd->htu", inner, values) * same_tile).astype(jnp.bfloat16)
    query_linear = (
        narrow("htu,uhd->thd", back, keys)
        + wide("the,hde->thd", inner_wide, incoming) * carried_prev[:, None, None]
    )
    tile_sum = narrow(
        "thd,the->hde", jnp.where(keep_first, queries, jnp.zeros_like(queries)), inner
    )
    key_soft, value_soft = parts[SPAN]
    if returned is None:
        returned = [
            from_behind(outgoing[shift - 1], "ctx", -shift) for shift in range(1, SPAN + 1)
        ]
    part = tile_sum
    covered = 1
    while 2 * covered < need:
        (flag,) = back_flags(doc_lengths, [(place, place + covered - 1)], tile)
        received = send_state(part, "ctx", -covered)
        if covered == 1:
            received, returned = lax.optimization_barrier((received, returned))
        part = part + (1.0 - flag) * received
        covered *= 2
    for moved in returned:
        key_soft = key_soft + moved[0].astype(jnp.float32)
        value_soft = value_soft + moved[1].astype(jnp.float32)
    later = send_state(part, "ctx", -1)
    if covered < need:
        (flag,) = back_flags(doc_lengths, [(place + 1, place + covered)], tile)
        later = later + (1.0 - flag) * send_state(part, "ctx", -1 - covered)
    key_linear = (
        narrow("htu,thd->uhd", back, queries)
        + wide("uhe,hde->uhd", values.astype(jnp.float32), later) * carried_next[:, None, None]
    )
    value_linear = (
        narrow("htu,the->uhe", attend, inner)
        + wide("uhd,hde->uhe", keys.astype(jnp.float32), later) * carried_next[:, None, None]
    )
    query_grad = (query_linear + query_soft).astype(jnp.bfloat16)
    key_grad = (key_linear + key_soft).astype(jnp.bfloat16)
    value_grad = (value_linear + value_soft).astype(jnp.bfloat16)
    return (mixed, query_grad, key_grad, value_grad)


def solution(mesh):
    placed = (
        P("ctx", "head", None),
        P("ctx", "head", None),
        P("ctx", "head", None),
        P("head", None),
        P(),
        P("ctx", "head", None),
    )
    return jax.shard_map(
        per_device,
        mesh=mesh,
        in_specs=placed,
        out_specs=(
            P("ctx", "head", None),
            P("ctx", "head", None),
            P("ctx", "head", None),
            P("ctx", "head", None),
        ),
        check_vma=False,
    )
```

```python
import jax
import jax.numpy as jnp
from jax import lax
from jax.sharding import PartitionSpec as P

SPAN = 2
MAXDOC = 2048


neg_large = -1e30
norm_eps = 1e-06


def from_behind(x, axis, by):
    devices = lax.axis_size(axis)
    pairs = [(i, i + by) for i in range(devices) if 0 <= i + by < devices]
    return lax.ppermute(x, axis, pairs)


def send_state(x, axis, by):
    return from_behind(x.astype(jnp.bfloat16), axis, by).astype(jnp.float32)


def tile_state(keys_t, values_t, doc_lengths, start):
    tile = keys_t.shape[0]
    docs = doc_index(doc_lengths, start + jnp.arange(tile, dtype=jnp.int32))
    keep = (docs == docs[tile - 1])[:, None, None]
    return narrow("uhd,uhe->hde", jnp.where(keep, keys_t, jnp.zeros_like(keys_t)), values_t)


def fold_states(pieces, flags):
    total = pieces[0]
    for piece, flag in zip(pieces[1:], flags[1:]):
        total = piece + (1.0 - flag) * total
    return total


def front_flags(doc_lengths, spans, tile):
    low = jnp.stack([lo * tile - 1 for lo, hi in spans])
    high = jnp.stack([hi * tile + tile - 1 for lo, hi in spans])
    docs = doc_index(doc_lengths, jnp.concatenate([low, high]).astype(jnp.int32))
    count = len(spans)
    return (docs[:count] != docs[count:]).astype(jnp.float32)


def back_flags(doc_lengths, spans, tile):
    low = jnp.stack([lo * tile for lo, hi in spans])
    high = jnp.stack([hi * tile + tile for lo, hi in spans])
    docs = doc_index(doc_lengths, jnp.concatenate([low, high]).astype(jnp.int32))
    count = len(spans)
    return (docs[:count] != docs[count:]).astype(jnp.float32)


def wide(form, left, right):
    return jnp.einsum(form, left, right, precision=lax.Precision.HIGHEST)


def narrow(form, left, right):
    return jnp.einsum(form, left, right, preferred_element_type=jnp.float32)


def doc_index(doc_lengths, positions):
    starts = jnp.cumsum(doc_lengths) - doc_lengths
    return jnp.sum((starts[None, :] <= positions[:, None]).astype(jnp.int32), axis=1) - 1


def one_doc(doc_lengths, position):
    return doc_index(doc_lengths, jnp.reshape(position, (1,)))[0]


def masked_scores(query_block, key_block, mask, scale):
    raw = narrow("thd,uhd->htu", query_block, key_block) * scale
    return jnp.where(mask[None], raw, neg_large)


def key_terms(dscores, weights, query_block, grad_block, scale):
    key_part = narrow("htu,thd->uhd", dscores, query_block) * scale
    value_part = narrow("htu,thd->uhd", weights, grad_block)
    return (key_part, value_part)


def per_device(queries, keys, values, gain, doc_lengths, cotangent):
    tile, heads, width = queries.shape
    features = heads * lax.axis_size("head") * width
    scale = width ** (-0.5)
    base = lax.axis_index("ctx") * tile
    offsets = jnp.arange(tile, dtype=jnp.int32)
    own_pos = base + offsets
    own_doc = doc_index(doc_lengths, own_pos)
    prev_doc = one_doc(doc_lengths, base - 1)
    next_doc = one_doc(doc_lengths, base + tile)
    pair = jnp.stack([keys, values])
    arrived = [from_behind(pair, "ctx", shift) for shift in range(SPAN, 0, -1)]
    key_tiles = [piece[0] for piece in arrived] + [keys]
    value_tiles = [piece[1] for piece in arrived] + [values]
    masks = []
    for position in range(SPAN + 1):
        key_pos = base - (SPAN - position) * tile + offsets
        key_doc = doc_index(doc_lengths, key_pos)
        masks.append(
            (own_doc[:, None] == key_doc[None, :]) & (key_pos[None, :] <= own_pos[:, None])
        )
    score_list = [
        masked_scores(queries, key_tiles[position], masks[position], scale)
        for position in range(SPAN + 1)
    ]
    top = score_list[0].max(axis=-1)
    for position in range(1, SPAN + 1):
        top = jnp.maximum(top, score_list[position].max(axis=-1))
    total = jnp.zeros((heads, tile), jnp.float32)
    for position in range(SPAN + 1):
        total = total + jnp.sum(jnp.exp(score_list[position] - top[..., None]), axis=-1)
    log_total = top + jnp.log(total)
    prob_list = []
    weight_list = []
    soft_out = jnp.zeros((tile, heads, width), jnp.float32)
    for position in range(SPAN + 1):
        probs = jnp.exp(score_list[position] - log_total[..., None])
        weights = probs.astype(jnp.bfloat16)
        prob_list.append(probs)
        weight_list.append(weights)
        soft_out = soft_out + narrow("htu,uhd->thd", weights, value_tiles[position])
    same_tile = masks[SPAN].astype(jnp.float32)
    carried_prev = (own_doc == prev_doc).astype(jnp.float32)
    carried_next = (own_doc == next_doc).astype(jnp.float32)
    keep_first = (own_doc == own_doc[0])[:, None, None]
    query_wide = queries.astype(jnp.float32)
    attend = (narrow("thd,uhd->htu", queries, keys) * same_tile).astype(jnp.bfloat16)
    grad_wide = cotangent.astype(jnp.float32)
    row_dot = jnp.sum(grad_wide * soft_out, axis=-1).T
    query_soft = jnp.zeros((tile, heads, width), jnp.float32)
    dscore_list = []
    for position in range(SPAN + 1):
        dprobs = narrow("thd,uhd->htu", cotangent, value_tiles[position])
        dscores = (prob_list[position] * (dprobs - row_dot[..., None])).astype(jnp.bfloat16)
        query_soft = query_soft + narrow("htu,uhd->thd", dscores, key_tiles[position]) * scale
        dscore_list.append(dscores)
    parts = [
        key_terms(dscore_list[position], weight_list[position], queries, cotangent, scale)
        for position in range(SPAN + 1)
    ]
    outgoing = [
        jnp.stack(list(parts[SPAN - shift])).astype(jnp.bfloat16) for shift in range(1, SPAN + 1)
    ]
    place = lax.axis_index("ctx")
    need = min(-(-MAXDOC // tile), lax.axis_size("ctx"))
    near_states = [
        tile_state(key_tiles[position], value_tiles[position], doc_lengths,
                   base - (SPAN - position) * tile)
        for position in range(SPAN)
    ]
    near_spans = [(place - SPAN + position, place - SPAN + position) for position in range(SPAN)]
    incoming = fold_states(near_states, front_flags(doc_lengths, near_spans, tile))
    covered = SPAN
    returned = None
    while covered < need:
        (flag,) = front_flags(doc_lengths, [(place - covered, place - 1)], tile)
        if 2 * covered >= need:
            incoming, outgoing = lax.optimization_barrier((incoming, outgoing))
            returned = [
                from_behind(outgoing[shift - 1], "ctx", -shift) for shift in range(1, SPAN + 1)
            ]
        incoming = incoming + (1.0 - flag) * send_state(incoming, "ctx", covered)
        covered *= 2
    linear_out = (
        narrow("htu,uhd->thd", attend, values)
        + wide("thd,hde->the", query_wide, incoming) * carried_prev[:, None, None]
    )
    weighted = cotangent.astype(jnp.float32) * gain[None]
    squares, projection = lax.psum(
        jnp.stack([
            jnp.sum(linear_out * linear_out, axis=(1, 2)),
            jnp.sum(weighted * linear_out, axis=(1, 2)),
        ]),
        "head",
    )
    inverse = lax.rsqrt(squares / features + norm_eps)
    mixed = (linear_out * inverse[:, None, None] * gain[None] + soft_out).astype(jnp.bfloat16)
    inner = (
        inverse[:, None, None] * weighted
        - linear_out * (inverse**3 * projection / features)[:, None, None]
    ).astype(jnp.bfloat16)
    inner_wide = inner.astype(jnp.float32)
    back = (narrow("thd,uhd->htu", inner, values) * same_tile).astype(jnp.bfloat16)
    query_linear = (
        narrow("htu,uhd->thd", back, keys)
        + wide("the,hde->thd", inner_wide, incoming) * carried_prev[:, None, None]
    )
    tile_sum = narrow(
        "thd,the->hde", jnp.where(keep_first, queries, jnp.zeros_like(queries)), inner
    )
    key_soft, value_soft = parts[SPAN]
    if returned is None:
        returned = [
            from_behind(outgoing[shift - 1], "ctx", -shift) for shift in range(1, SPAN + 1)
        ]
    part = tile_sum
    covered = 1
    while 2 * covered < need:
        (flag,) = back_flags(doc_lengths, [(place, place + covered - 1)], tile)
        received = send_state(part, "ctx", -covered)
        if covered == 1:
            received, returned = lax.optimization_barrier((received, returned))
        part = part + (1.0 - flag) * received
        covered *= 2
    for moved in returned:
        key_soft = key_soft + moved[0].astype(jnp.float32)
        value_soft = value_soft + moved[1].astype(jnp.float32)
    later = send_state(part, "ctx", -1)
    if covered < need:
        (flag,) = back_flags(doc_lengths, [(place + 1, place + covered)], tile)
        later = later + (1.0 - flag) * send_state(part, "ctx", -1 - covered)
    key_linear = (
        narrow("htu,thd->uhd", back, queries)
        + wide("uhe,hde->uhd", values.astype(jnp.float32), later) * carried_next[:, None, None]
    )
    value_linear = (
        narrow("htu,the->uhe", attend, inner)
        + wide("uhd,hde->uhe", keys.astype(jnp.float32), later) * carried_next[:, None, None]
    )
    query_grad = (query_linear + query_soft).astype(jnp.bfloat16)
    key_grad = (key_linear + key_soft).astype(jnp.bfloat16)
    value_grad = (value_linear + value_soft).astype(jnp.bfloat16)
    return (mixed, query_grad, key_grad, value_grad)


def solution(mesh):
    placed = (
        P("ctx", "head", None),
        P("ctx", "head", None),
        P("ctx", "head", None),
        P("head", None),
        P(),
        P("ctx", "head", None),
    )
    return jax.shard_map(
        per_device,
        mesh=mesh,
        in_specs=placed,
        out_specs=(
            P("ctx", "head", None),
            P("ctx", "head", None),
            P("ctx", "head", None),
            P("ctx", "head", None),
        ),
        check_vma=False,
    )
```
